32 devices in a mesh: energy: 8 (over y, x, core), space: 4 (over z).
Axes of the slice: x: 2, y: 2, z: 4, core: 2. Of those that a mesh axis runs over, the one named last changes fastest.
Arguments:
- g_lesser: bfloat16 [4, 2, 32, 16384], P('space', None, 'energy'), may hold values from -6 to 6
- g_greater: bfloat16 [4, 2, 32, 16384], P('space', None, 'energy'), may hold values from -6 to 6
- v_diag: float32 [4, 128, 128], P('space'), may hold values from -0.5 to 0.5
- v_couple: float32 [4, 128, 128], P('space'), may hold values from -0.5 to 0.5
Outputs:
- screened: float32 [4, 2, 32, 16384], P('space', None, 'energy')
The draws below stay inside these ranges and needn't reach their ends.
All inputs are finite; a program needn't handle non-finite values.
Results may differ from the reference program's by a relative error of at most 0.0003.
Values may be sent and summed in bfloat16 or wider, within the bound.
No kernel may reach another device: no remote copies, remote signals or barrier semaphores. Data moves between devices by JAX's collectives and lax.ppermute only.
A program may use at most 64 MiB of HBM per device.

```python
import jax
import jax.numpy as jnp
from jax import lax

BS = 128
E = 32
NB = 4
ELEMS = 16384


def block_scale(rng, extent, shards, least, high):
    factor_of = 1.0
    for dim, blocks in shards:
        steps = jax.random.uniform(jax.random.fold_in(jax.random.fold_in(rng, 6), dim), (blocks,), jnp.float32, least / len(shards), high / len(shards))
        factor_of = factor_of * jnp.repeat(jnp.exp(steps), extent[dim] // blocks).reshape((-1,) + (1,) * (len(extent) - 1 - dim))
    return factor_of


def gaussian(key, shape, scale, most, cuts=(), held_as=jnp.bfloat16):
    array = scale * jax.random.normal(key, shape, jnp.float32)
    if cuts:
        array = array * block_scale(key, shape, cuts, -0.22, 0.18)
    return jnp.clip(array, -most, most).astype(held_as)


def setup_inputs(seed: int = 0) -> dict:
    streams_of = jax.random.split(jax.random.key(seed), 5)
    g_lesser = gaussian(streams_of[0], (NB, 2, E, ELEMS), 1.0, 6.0, ((0, 4), (2, 8)))
    g_greater = gaussian(streams_of[1], (NB, 2, E, ELEMS), 1.0, 6.0, ((0, 4), (2, 8)))
    v_diag = gaussian(streams_of[2], (NB, BS, BS), BS ** -0.5, 0.5, ((0, 4),), jnp.float32)
    v_couple = gaussian(streams_of[3], (NB, BS, BS), BS ** -0.5, 0.5, ((0, 4),), jnp.float32)
    return dict(g_lesser=g_lesser, g_greater=g_greater, v_diag=v_diag, v_couple=v_couple)


def correlate_block(lesser, greater):
    first = lesser.astype(jnp.float32)
    second = greater.astype(jnp.float32)
    left = lax.complex(first[0], first[1])
    right = lax.complex(second[0], second[1])
    spectrum_left = jnp.fft.fft(left, n=2 * E, axis=0)
    spectrum_right = jnp.fft.fft(right, n=2 * E, axis=0)
    corr = jnp.fft.ifft(spectrum_left * jnp.conj(spectrum_right), axis=0)[:E]
    scale = E ** -0.5
    return jnp.stack([-scale * jnp.imag(corr), scale * jnp.real(corr)]).astype(jnp.float32)


def sandwich(left, field, right):
    shaped = field.reshape(2, E, BS, BS)
    inner = jnp.matmul(left, shaped, precision=lax.Precision.HIGHEST)
    outer = jnp.matmul(inner, right, precision=lax.Precision.HIGHEST)
    return outer.reshape(2, E, ELEMS)


def reference(g_lesser, g_greater, v_diag, v_couple):
    polar = lax.map(lambda pair: correlate_block(pair[0], pair[1]), (g_lesser, g_greater))

    def one_block(index):
        below = jnp.maximum(index - 1, 0)
        above = jnp.minimum(index + 1, NB - 1)
        local = sandwich(v_diag[index], polar[index], v_diag[index])
        from_below = sandwich(v_couple[below].T, polar[below], v_couple[below])
        from_above = sandwich(v_couple[index], polar[above], v_couple[index].T)
        has_below = (index > 0).astype(jnp.float32)
        has_above = (index < NB - 1).astype(jnp.float32)
        return local + has_below * from_below + has_above * from_above

    return lax.map(one_block, jnp.arange(NB, dtype=jnp.int32))
```

```python
import math

import jax
import jax.numpy as jnp
from jax import lax
from jax.sharding import PartitionSpec as P

BS = 128
QUANT = 128


def shifted(x, axis, by):
    devices = lax.axis_size(axis)
    pairs = [(i, i + by) for i in range(devices) if 0 <= i + by < devices]
    return lax.ppermute(x, axis, pairs)


def product(left, right):
    return jnp.dot(left, right, precision=lax.Precision.HIGHEST, preferred_element_type=jnp.float32)


def complex_apply(real_table, sum_table, diff_table, re_part, im_part):
    first = product(real_table, re_part + im_part)
    second = product(sum_table, im_part)
    third = product(diff_table, re_part)
    return (first - second, first + third)


def correlate(both_re, both_im, count, width):
    length = 2 * count
    rows = lax.iota(jnp.int32, length)[:, None]
    cols = lax.iota(jnp.int32, count)[None, :]
    phase = (rows * cols % length).astype(jnp.float32) * (2.0 * math.pi / length)
    cosine = jnp.cos(phase)
    sine = jnp.sin(phase)
    fwd_sum = cosine - sine
    fwd_diff = -sine - cosine
    s_re, s_im = complex_apply(cosine, fwd_sum, fwd_diff, both_re, both_im)
    l_re = s_re[:, :width]
    l_im = s_im[:, :width]
    g_re = s_re[:, width:]
    g_im = s_im[:, width:]
    z_re = l_re * g_re + l_im * g_im
    z_im = l_im * g_re - l_re * g_im
    inv_cos = cosine.T / length
    inv_sin = sine.T / length
    c_re, c_im = complex_apply(inv_cos, inv_cos + inv_sin, inv_sin - inv_cos, z_re, z_im)
    scale = count ** (-0.5)
    return jnp.stack([-scale * c_im, scale * c_re])


def sandwich(left, field, right):
    inner = jnp.matmul(left, field, precision=lax.Precision.HIGHEST)
    return jnp.matmul(inner, right, precision=lax.Precision.HIGHEST)


def per_device(g_lesser, g_greater, v_diag, v_couple):
    groups = lax.axis_size("energy")
    e_local = g_lesser.shape[2]
    elements = g_lesser.shape[3]
    count = e_local * groups
    tile_width = (elements + groups * QUANT - 1) // (groups * QUANT) * QUANT
    padding = tile_width * groups - elements

    couple_own = v_couple[0]
    couple_prev = shifted(couple_own, "space", 1)

    both = jnp.stack([g_lesser[0], g_greater[0]])
    both = jnp.pad(both, ((0, 0), (0, 0), (0, 0), (0, padding)))
    both = both.reshape(2, 2, e_local, groups, tile_width)
    both = both.transpose(3, 0, 1, 2, 4).reshape(groups, 4 * e_local, tile_width)
    got = lax.all_to_all(both, "energy", 0, 0, tiled=True)
    got = got.reshape(groups, 2, 2, e_local, tile_width).astype(jnp.float32)
    got = got.transpose(2, 0, 3, 1, 4).reshape(2, count, 2 * tile_width)
    polar_tile = correlate(got[0], got[1], count, tile_width)

    send = polar_tile.reshape(2, groups, e_local, tile_width).transpose(1, 0, 2, 3)
    send = send.reshape(groups, 2 * e_local, tile_width)
    back = lax.all_to_all(send, "energy", 0, 0, tiled=True)
    back = back.reshape(groups, 2, e_local, tile_width).transpose(1, 2, 0, 3)
    back = back.reshape(2, e_local, groups * tile_width)[:, :, :elements]
    polar = back.reshape(2, e_local, BS, BS)

    diag_block = v_diag[0]
    to_next = sandwich(couple_own.T, polar, couple_own)
    to_prev = sandwich(couple_prev, polar, couple_prev.T)
    from_below = shifted(to_next, "space", 1)
    from_above = shifted(to_prev, "space", -1)
    local = sandwich(diag_block, polar, diag_block)
    total = local + from_below + from_above
    return total.reshape(1, 2, e_local, elements)


def solution(mesh):
    placed = (
        P("space", None, "energy", None),
        P("space", None, "energy", None),
        P("space", None, None),
        P("space", None, None),
    )
    return jax.shard_map(
        per_device,
        mesh=mesh,
        in_specs=placed,
        out_specs=P("space", None, "energy", None),
        check_vma=False,
    )
```

```python
import math

import jax
import jax.numpy as jnp
from jax import lax
from jax.sharding import PartitionSpec as P

BS = 128
QUANT = 128


def shifted(x, axis, by):
    devices = lax.axis_size(axis)
    pairs = [(i, i + by) for i in range(devices) if 0 <= i + by < devices]
    return lax.ppermute(x, axis, pairs)


def tables(count, e_local, groups):
    length = 2 * count
    k = lax.iota(jnp.int32, length)
    n = lax.iota(jnp.int32, count)
    phase = ((k[:, None] * n[None, :]) % length).astype(jnp.float32) * (2.0 * math.pi / length)
    cosine = jnp.cos(phase)
    sine = jnp.sin(phase)
    re_rows = jnp.stack([cosine, sine], axis=1)
    im_rows = jnp.stack([-sine, cosine], axis=1)
    per_part = jnp.stack([re_rows, im_rows])
    per_part = per_part.reshape(2, length, 2, groups, e_local).transpose(0, 1, 3, 2, 4)
    zero = jnp.zeros_like(per_part)
    lesser_rows = jnp.stack([per_part, zero], axis=3)
    greater_rows = jnp.stack([zero, per_part], axis=3)
    forward = jnp.stack([lesser_rows, greater_rows]).reshape(4 * length, 4 * count)
    scale = count ** (-0.5) / length
    inv_cos = cosine.T * scale
    inv_sin = sine.T * scale
    ri0 = jnp.concatenate([-inv_sin, -inv_cos], axis=1)
    ri1 = jnp.concatenate([inv_cos, -inv_sin], axis=1)
    inverse = jnp.stack([ri0, ri1]).reshape(2, groups, e_local, 2 * length)
    inverse = inverse.transpose(1, 0, 2, 3).reshape(2 * count, 2 * length)
    return forward, inverse


def correlate(got, forward, inverse):
    high = lax.reduce_precision(forward, exponent_bits=8, mantissa_bits=7)
    low = forward - high
    split = jnp.concatenate([high, low]).astype(jnp.bfloat16)
    both = jnp.dot(split, got, preferred_element_type=jnp.float32)
    rows = forward.shape[0]
    spectrum = both[:rows] + both[rows:]
    length = rows // 4
    l_re, l_im, g_re, g_im = (spectrum[i * length:(i + 1) * length] for i in range(4))
    z_re = l_re * g_re + l_im * g_im
    z_im = l_im * g_re - l_re * g_im
    z = jnp.concatenate([z_re, z_im])
    return jnp.dot(inverse, z, precision=lax.Precision.HIGHEST, preferred_element_type=jnp.float32)


def sandwich(left, field, right):
    inner = jnp.matmul(left, field, precision=lax.Precision.HIGHEST)
    return jnp.matmul(inner, right, precision=lax.Precision.HIGHEST)


def per_device(g_lesser, g_greater, v_diag, v_couple):
    groups = lax.axis_size("energy")
    e_local = g_lesser.shape[2]
    elements = g_lesser.shape[3]
    count = e_local * groups
    tile_width = (elements + groups * QUANT - 1) // (groups * QUANT) * QUANT
    padding = tile_width * groups - elements

    couple_own = v_couple[0]
    couple_prev = shifted(couple_own, "space", 1)
    forward, inverse = tables(count, e_local, groups)

    both = jnp.stack([g_lesser[0], g_greater[0]])
    both = jnp.pad(both, ((0, 0), (0, 0), (0, 0), (0, padding)))
    both = both.reshape(2, 2, e_local, groups, tile_width)
    both = both.transpose(3, 0, 1, 2, 4).reshape(groups, 4 * e_local, tile_width)
    got = lax.all_to_all(both, "energy", 0, 0, tiled=True)
    polar_tile = correlate(got.reshape(groups * 4 * e_local, tile_width), forward, inverse)

    send = polar_tile.reshape(groups, 2 * e_local, tile_width)
    back = lax.all_to_all(send, "energy", 0, 0, tiled=True)
    back = back.reshape(groups, 2, e_local, tile_width).transpose(1, 2, 0, 3)
    back = back.reshape(2, e_local, groups * tile_width)[:, :, :elements]
    polar = back.reshape(2, e_local, BS, BS)

    polar_below = shifted(polar, "space", 1)
    polar_above = shifted(polar, "space", -1)
    diag_block = v_diag[0]
    local = sandwich(diag_block, polar, diag_block)
    from_below = sandwich(couple_prev.T, polar_below, couple_prev)
    from_above = sandwich(couple_own, polar_above, couple_own.T)
    total = local + from_below + from_above
    return total.reshape(1, 2, e_local, elements)


def solution(mesh):
    placed = (
        P("space", None, "energy", None),
        P("space", None, "energy", None),
        P("space", None, None),
        P("space", None, None),
    )
    return jax.shard_map(
        per_device,
        mesh=mesh,
        in_specs=placed,
        out_specs=P("space", None, "energy", None),
        check_vma=False,
    )
```

```python
import math

import jax
import jax.numpy as jnp
from jax import lax
from jax.sharding import PartitionSpec as P

BS = 128
QUANT = 128


def shifted(x, axis, by):
    devices = lax.axis_size(axis)
    pairs = [(i, i + by) for i in range(devices) if 0 <= i + by < devices]
    return lax.ppermute(x, axis, pairs)


def tables(count, e_local, groups):
    length = 2 * count
    k = lax.iota(jnp.int32, length)
    n = lax.iota(jnp.int32, count)
    phase = ((k[:, None] * n[None, :]) % length).astype(jnp.float32) * (2.0 * math.pi / length)
    cosine = jnp.cos(phase)
    sine = jnp.sin(phase)
    re_rows = jnp.stack([cosine, sine], axis=1)
    im_rows = jnp.stack([-sine, cosine], axis=1)
    per_part = jnp.stack([re_rows, im_rows])
    per_part = per_part.reshape(2, length, 2, groups, e_local).transpose(0, 1, 3, 2, 4)
    zero = jnp.zeros_like(per_part)
    lesser_rows = jnp.stack([per_part, zero], axis=3)
    greater_rows = jnp.stack([zero, per_part], axis=3)
    forward = jnp.stack([lesser_rows, greater_rows]).reshape(4 * length, 4 * count)
    scale = count ** (-0.5) / length
    inv_cos = cosine.T * scale
    inv_sin = sine.T * scale
    ri0 = jnp.concatenate([-inv_sin, -inv_cos], axis=1)
    ri1 = jnp.concatenate([inv_cos, -inv_sin], axis=1)
    inverse = jnp.stack([ri0, ri1]).reshape(2, groups, e_local, 2 * length)
    inverse = inverse.transpose(1, 0, 2, 3).reshape(2 * count, 2 * length)
    return forward, inverse


def correlate(got, forward, inverse):
    high = lax.reduce_precision(forward, exponent_bits=8, mantissa_bits=7)
    low = forward - high
    split = jnp.concatenate([high, low]).astype(jnp.bfloat16)
    both = jnp.dot(split, got, preferred_element_type=jnp.float32)
    rows = forward.shape[0]
    spectrum = both[:rows] + both[rows:]
    length = rows // 4
    l_re, l_im, g_re, g_im = (spectrum[i * length:(i + 1) * length] for i in range(4))
    z_re = l_re * g_re + l_im * g_im
    z_im = l_im * g_re - l_re * g_im
    z = jnp.concatenate([z_re, z_im])
    return jnp.dot(inverse, z, precision=lax.Precision.HIGHEST, preferred_element_type=jnp.float32)


def sandwich(left, field, right):
    inner = jnp.matmul(left, field, precision=lax.Precision.HIGHEST)
    return jnp.matmul(inner, right, precision=lax.Precision.HIGHEST)


def per_device(g_lesser, g_greater, v_diag, v_couple):
    groups = lax.axis_size("energy")
    e_local = g_lesser.shape[2]
    elements = g_lesser.shape[3]
    count = e_local * groups
    tile_width = (elements + groups * QUANT - 1) // (groups * QUANT) * QUANT
    padding = tile_width * groups - elements

    couple_own = v_couple[0]
    forward, inverse = tables(count, e_local, groups)

    both = jnp.stack([g_lesser[0], g_greater[0]])
    both = jnp.pad(both, ((0, 0), (0, 0), (0, 0), (0, padding)))
    both = both.reshape(2, 2, e_local, groups, tile_width)
    both = both.transpose(3, 0, 1, 2, 4).reshape(groups, 4 * e_local, tile_width)
    got = lax.all_to_all(both, "energy", 0, 0, tiled=True)
    polar_tile = correlate(got.reshape(groups * 4 * e_local, tile_width), forward, inverse)

    send = polar_tile.reshape(groups, 2 * e_local, tile_width)
    back = lax.all_to_all(send, "energy", 0, 0, tiled=True)
    back = back.reshape(groups, 2, e_local, tile_width).transpose(1, 2, 0, 3)
    back = back.reshape(2, e_local, groups * tile_width)[:, :, :elements]
    polar = back.reshape(2, e_local, BS, BS)

    diag_block = v_diag[0]
    polar_above = shifted(polar, "space", -1)
    to_next = sandwich(couple_own.T, polar, couple_own)
    from_below = shifted(to_next, "space", 1)
    local = sandwich(diag_block, polar, diag_block)
    from_above = sandwich(couple_own, polar_above, couple_own.T)
    total = local + from_below + from_above
    return total.reshape(1, 2, e_local, elements)


def solution(mesh):
    placed = (
        P("space", None, "energy", None),
        P("space", None, "energy", None),
        P("space", None, None),
        P("space", None, None),
    )
    return jax.shard_map(
        per_device,
        mesh=mesh,
        in_specs=placed,
        out_specs=P("space", None, "energy", None),
        check_vma=False,
    )
```

```python
import math

import jax
import jax.numpy as jnp
from jax import lax
from jax.sharding import PartitionSpec as P

BS = 128
QUANT = 128


def shifted(x, axis, by):
    devices = lax.axis_size(axis)
    pairs = [(i, i + by) for i in range(devices) if 0 <= i + by < devices]
    return lax.ppermute(x, axis, pairs)


def tables(count, e_local, groups):
    length = 2 * count
    k = lax.iota(jnp.int32, length)
    n = lax.iota(jnp.int32, count)
    phase = ((k[:, None] * n[None, :]) % length).astype(jnp.float32) * (2.0 * math.pi / length)
    cosine = jnp.cos(phase)
    sine = jnp.sin(phase)
    re_rows = jnp.stack([cosine, sine], axis=1)
    im_rows = jnp.stack([-sine, cosine], axis=1)
    per_part = jnp.stack([re_rows, im_rows])
    per_part = per_part.reshape(2, length, 2, groups, e_local).transpose(0, 1, 3, 2, 4)
    zero = jnp.zeros_like(per_part)
    lesser_rows = jnp.stack([per_part, zero], axis=3)
    greater_rows = jnp.stack([zero, per_part], axis=3)
    forward = jnp.stack([lesser_rows, greater_rows]).reshape(4 * length, 4 * count)
    scale = count ** (-0.5) / length
    inv_cos = cosine.T * scale
    inv_sin = sine.T * scale
    ri0 = jnp.concatenate([-inv_sin, -inv_cos], axis=1)
    ri1 = jnp.concatenate([inv_cos, -inv_sin], axis=1)
    inverse = jnp.stack([ri0, ri1]).reshape(2, groups, e_local, 2 * length)
    inverse = inverse.transpose(1, 0, 2, 3).reshape(2 * count, 2 * length)
    return forward, inverse


def correlate(got, forward, inverse):
    high = lax.reduce_precision(forward, exponent_bits=8, mantissa_bits=7)
    low = forward - high
    split = jnp.concatenate([high, low]).astype(jnp.bfloat16)
    both = jnp.dot(split, got, preferred_element_type=jnp.float32)
    rows = forward.shape[0]
    spectrum = both[:rows] + both[rows:]
    length = rows // 4
    l_re, l_im, g_re, g_im = (spectrum[i * length:(i + 1) * length] for i in range(4))
    z_re = l_re * g_re + l_im * g_im
    z_im = l_im * g_re - l_re * g_im
    z = jnp.concatenate([z_re, z_im])
    return jnp.dot(inverse, z, precision=lax.Precision.HIGHEST, preferred_element_type=jnp.float32)


def sandwich(left, field, right):
    inner = jnp.matmul(left, field, precision=lax.Precision.HIGHEST)
    return jnp.matmul(inner, right, precision=lax.Precision.HIGHEST)


def per_device(g_lesser, g_greater, v_diag, v_couple):
    groups = lax.axis_size("energy")
    e_local = g_lesser.shape[2]
    elements = g_lesser.shape[3]
    count = e_local * groups
    tile_width = (elements + groups * QUANT - 1) // (groups * QUANT) * QUANT
    padding = tile_width * groups - elements

    couple_own = v_couple[0]
    couple_prev = shifted(couple_own, "space", 1)
    forward, inverse = tables(count, e_local, groups)

    def by_destination(part):
        part = jnp.pad(part[0], ((0, 0), (0, 0), (0, padding)))
        return part.reshape(2, e_local, groups, tile_width).transpose(2, 0, 1, 3)

    both = jnp.concatenate([by_destination(g_lesser), by_destination(g_greater)], axis=1)
    both, couple_prev = lax.optimization_barrier((both, couple_prev))
    got = lax.all_to_all(both, "energy", 0, 0, tiled=True)
    polar_tile = correlate(got.reshape(groups * 4 * e_local, tile_width), forward, inverse)

    send = polar_tile.reshape(groups, 2 * e_local, tile_width)
    back = lax.all_to_all(send, "energy", 0, 0, tiled=True)
    back = back.reshape(groups, 2, e_local, tile_width).transpose(1, 2, 0, 3)
    back = back.reshape(2, e_local, groups * tile_width)[:, :, :elements]
    polar = back.reshape(2, e_local, BS, BS)

    diag_block = v_diag[0]
    polar_above = shifted(polar, "space", -1)
    polar_below = shifted(polar, "space", 1)
    local = sandwich(diag_block, polar, diag_block)
    from_below = sandwich(couple_prev.T, polar_below, couple_prev)
    from_above = sandwich(couple_own, polar_above, couple_own.T)
    total = local + from_below + from_above
    return total.reshape(1, 2, e_local, elements)


def solution(mesh):
    placed = (
        P("space", None, "energy", None),
        P("space", None, "energy", None),
        P("space", None, None),
        P("space", None, None),
    )
    return jax.shard_map(
        per_device,
        mesh=mesh,
        in_specs=placed,
        out_specs=P("space", None, "energy", None),
        check_vma=False,
    )
```

```python
import math

import jax
import jax.numpy as jnp
from jax import lax
from jax.sharding import PartitionSpec as P

BS = 128
QUANT = 128


def shifted(x, axis, by):
    devices = lax.axis_size(axis)
    pairs = [(i, i + by) for i in range(devices) if 0 <= i + by < devices]
    return lax.ppermute(x, axis, pairs)


def tables(count, e_local, groups):
    length = 2 * count
    k = lax.iota(jnp.int32, length)
    n = lax.iota(jnp.int32, count)
    phase = ((k[:, None] * n[None, :]) % length).astype(jnp.float32) * (2.0 * math.pi / length)
    cosine = jnp.cos(phase)
    sine = jnp.sin(phase)
    re_rows = jnp.stack([cosine, sine], axis=1)
    im_rows = jnp.stack([-sine, cosine], axis=1)
    per_part = jnp.stack([re_rows, im_rows])
    per_part = per_part.reshape(2, length, 2, groups, e_local).transpose(0, 1, 3, 2, 4)
    zero = jnp.zeros_like(per_part)
    lesser_rows = jnp.stack([per_part, zero], axis=3)
    greater_rows = jnp.stack([zero, per_part], axis=3)
    forward = jnp.stack([lesser_rows, greater_rows]).reshape(4 * length, 4 * count)
    scale = count ** (-0.5) / length
    inv_cos = cosine.T * scale
    inv_sin = sine.T * scale
    ri0 = jnp.concatenate([-inv_sin, -inv_cos], axis=1)
    ri1 = jnp.concatenate([inv_cos, -inv_sin], axis=1)
    inverse = jnp.stack([ri0, ri1]).reshape(2, groups, e_local, 2 * length)
    inverse = inverse.transpose(1, 0, 2, 3).reshape(2 * count, 2 * length)
    return forward, inverse


def correlate(got, forward, inverse):
    high = lax.reduce_precision(forward, exponent_bits=8, mantissa_bits=7)
    low = forward - high
    split = jnp.concatenate([high, low]).astype(jnp.bfloat16)
    both = jnp.dot(split, got, preferred_element_type=jnp.float32)
    rows = forward.shape[0]
    spectrum = both[:rows] + both[rows:]
    length = rows // 4
    l_re, l_im, g_re, g_im = (spectrum[i * length:(i + 1) * length] for i in range(4))
    z_re = l_re * g_re + l_im * g_im
    z_im = l_im * g_re - l_re * g_im
    z = jnp.concatenate([z_re, z_im])
    return jnp.dot(inverse, z, precision=lax.Precision.HIGHEST, preferred_element_type=jnp.float32)


def sandwich(left, field, right):
    inner = jnp.matmul(left, field, precision=lax.Precision.HIGH)
    return jnp.matmul(inner, right, precision=lax.Precision.HIGH)


def per_device(g_lesser, g_greater, v_diag, v_couple):
    groups = lax.axis_size("energy")
    e_local = g_lesser.shape[2]
    elements = g_lesser.shape[3]
    count = e_local * groups
    tile_width = (elements + groups * QUANT - 1) // (groups * QUANT) * QUANT
    padding = tile_width * groups - elements

    couple_own = v_couple[0]
    forward, inverse = tables(count, e_local, groups)

    both = jnp.stack([g_lesser[0], g_greater[0]])
    both = jnp.pad(both, ((0, 0), (0, 0), (0, 0), (0, padding)))
    both = both.reshape(2, 2, e_local, groups, tile_width)
    both = both.transpose(3, 0, 1, 2, 4).reshape(groups, 4 * e_local, tile_width)
    got = lax.all_to_all(both, "energy", 0, 0, tiled=True)
    polar_tile = correlate(got.reshape(groups * 4 * e_local, tile_width), forward, inverse)

    send = polar_tile.reshape(groups, 2 * e_local, tile_width)
    back = lax.all_to_all(send, "energy", 0, 0, tiled=True)
    back = back.reshape(groups, 2, e_local, tile_width).transpose(1, 2, 0, 3)
    back = back.reshape(2, e_local, groups * tile_width)[:, :, :elements]
    polar = back.reshape(2, e_local, BS, BS)

    diag_block = v_diag[0]
    polar_above = shifted(polar, "space", -1)
    to_next = sandwich(couple_own.T, polar, couple_own)
    from_below = shifted(to_next, "space", 1)
    local = sandwich(diag_block, polar, diag_block)
    from_above = sandwich(couple_own, polar_above, couple_own.T)
    local, from_below, from_above = lax.optimization_barrier((local, from_below, from_above))
    shape = (1, 2, e_local, elements)
    return local.reshape(shape) + from_below.reshape(shape) + from_above.reshape(shape)


def solution(mesh):
    placed = (
        P("space", None, "energy", None),
        P("space", None, "energy", None),
        P("space", None, None),
        P("space", None, None),
    )
    return jax.shard_map(
        per_device,
        mesh=mesh,
        in_specs=placed,
        out_specs=P("space", None, "energy", None),
        check_vma=False,
    )
```

```python
import math

import jax
import jax.numpy as jnp
from jax import lax
from jax.sharding import PartitionSpec as P

BS = 128
QUANT = 128


def shifted(x, axis, by):
    devices = lax.axis_size(axis)
    pairs = [(i, i + by) for i in range(devices) if 0 <= i + by < devices]
    return lax.ppermute(x, axis, pairs)


def tables(count, e_local, groups):
    length = 2 * count
    k = lax.iota(jnp.int32, length)
    n = lax.iota(jnp.int32, count)
    phase = ((k[:, None] * n[None, :]) % length).astype(jnp.float32) * (2.0 * math.pi / length)
    cosine = jnp.cos(phase)
    sine = jnp.sin(phase)
    re_rows = jnp.stack([cosine, sine], axis=1)
    im_rows = jnp.stack([-sine, cosine], axis=1)
    per_part = jnp.stack([re_rows, im_rows])
    per_part = per_part.reshape(2, length, 2, groups, e_local).transpose(0, 1, 3, 2, 4)
    zero = jnp.zeros_like(per_part)
    lesser_rows = jnp.stack([per_part, zero], axis=3)
    greater_rows = jnp.stack([zero, per_part], axis=3)
    forward = jnp.stack([lesser_rows, greater_rows]).reshape(4 * length, 4 * count)
    scale = count ** (-0.5) / length
    inv_cos = cosine.T * scale
    inv_sin = sine.T * scale
    ri0 = jnp.concatenate([-inv_sin, -inv_cos], axis=1)
    ri1 = jnp.concatenate([inv_cos, -inv_sin], axis=1)
    inverse = jnp.stack([ri0, ri1]).reshape(2, groups, e_local, 2 * length)
    inverse = inverse.transpose(1, 0, 2, 3).reshape(2 * count, 2 * length)
    return forward, inverse


def correlate(got, forward, inverse):
    high = lax.reduce_precision(forward, exponent_bits=8, mantissa_bits=7)
    low = forward - high
    spectrum = jnp.dot(high.astype(jnp.bfloat16), got, preferred_element_type=jnp.float32)
    spectrum = spectrum + jnp.dot(low.astype(jnp.bfloat16), got, preferred_element_type=jnp.float32)
    length = forward.shape[0] // 4
    l_re, l_im, g_re, g_im = (spectrum[i * length:(i + 1) * length] for i in range(4))
    z_re = l_re * g_re + l_im * g_im
    z_im = l_im * g_re - l_re * g_im
    z = jnp.concatenate([z_re, z_im])
    return jnp.dot(inverse, z, precision=lax.Precision.HIGH, preferred_element_type=jnp.float32)


def sandwich(left, field, right):
    inner = jnp.matmul(left, field, precision=lax.Precision.HIGH)
    return jnp.matmul(inner, right, precision=lax.Precision.HIGH)


def per_device(g_lesser, g_greater, v_diag, v_couple):
    groups = lax.axis_size("energy")
    e_local = g_lesser.shape[2]
    elements = g_lesser.shape[3]
    count = e_local * groups
    tile_width = (elements + groups * QUANT - 1) // (groups * QUANT) * QUANT
    padding = tile_width * groups - elements

    couple_own = v_couple[0]
    forward, inverse = tables(count, e_local, groups)

    both = jnp.stack([g_lesser[0], g_greater[0]])
    both = jnp.pad(both, ((0, 0), (0, 0), (0, 0), (0, padding)))
    both = both.reshape(2, 2, e_local, groups, tile_width)
    both = both.transpose(3, 0, 1, 2, 4).reshape(groups, 4 * e_local, tile_width)
    got = lax.all_to_all(both, "energy", 0, 0, tiled=True)
    polar_tile = correlate(got.reshape(groups * 4 * e_local, tile_width), forward, inverse)

    send = polar_tile.reshape(groups, 2 * e_local, tile_width)
    back = lax.all_to_all(send, "energy", 0, 0, tiled=True)
    back = back.reshape(groups, 2, e_local, tile_width).transpose(1, 2, 0, 3)
    back = back.reshape(2, e_local, groups * tile_width)[:, :, :elements]
    polar = back.reshape(2, e_local, BS, BS)

    diag_block = v_diag[0]
    polar_above = shifted(polar, "space", -1)
    to_next = sandwich(couple_own.T, polar, couple_own)
    from_below = shifted(to_next, "space", 1)
    local = sandwich(diag_block, polar, diag_block)
    from_above = sandwich(couple_own, polar_above, couple_own.T)
    local, from_below, from_above = lax.optimization_barrier((local, from_below, from_above))
    shape = (1, 2, e_local, elements)
    return local.reshape(shape) + from_below.reshape(shape) + from_above.reshape(shape)


def solution(mesh):
    placed = (
        P("space", None, "energy", None),
        P("space", None, "energy", None),
        P("space", None, None),
        P("space", None, None),
    )
    return jax.shard_map(
        per_device,
        mesh=mesh,
        in_specs=placed,
        out_specs=P("space", None, "energy", None),
        check_vma=False,
    )
```

```python
import math

import jax
import jax.numpy as jnp
from jax import lax
from jax.experimental import pallas as pl
from jax.experimental.pallas import tpu as pltpu
from jax.sharding import PartitionSpec as P

BS = 128
QUANT = 128


def shifted(x, axis, by):
    devices = lax.axis_size(axis)
    pairs = [(i, i + by) for i in range(devices) if 0 <= i + by < devices]
    return lax.ppermute(x, axis, pairs)


def tables(count, e_local, groups):
    length = 2 * count
    k = lax.iota(jnp.int32, length)
    n = lax.iota(jnp.int32, count)
    phase = ((k[:, None] * n[None, :]) % length).astype(jnp.float32) * (2.0 * math.pi / length)
    cosine = jnp.cos(phase)
    sine = jnp.sin(phase)
    re_rows = jnp.stack([cosine, sine], axis=1)
    im_rows = jnp.stack([-sine, cosine], axis=1)
    per_part = jnp.stack([re_rows, im_rows])
    per_part = per_part.reshape(2, length, 2, groups, e_local).transpose(0, 1, 3, 2, 4)
    zero = jnp.zeros_like(per_part)
    lesser_rows = jnp.stack([per_part, zero], axis=3)
    greater_rows = jnp.stack([zero, per_part], axis=3)
    forward = jnp.stack([lesser_rows, greater_rows]).reshape(4 * length, 4 * count)
    scale = count ** (-0.5) / length
    inv_cos = cosine.T * scale
    inv_sin = sine.T * scale
    ri0 = jnp.concatenate([-inv_sin, -inv_cos], axis=1)
    ri1 = jnp.concatenate([inv_cos, -inv_sin], axis=1)
    inverse = jnp.stack([ri0, ri1]).reshape(2, groups, e_local, 2 * length)
    inverse = inverse.transpose(1, 0, 2, 3).reshape(2 * count, 2 * length)
    return forward, inverse


def correlate(got, forward, inverse):
    high = lax.reduce_precision(forward, exponent_bits=8, mantissa_bits=7)
    low = forward - high
    spectrum = jnp.dot(high.astype(jnp.bfloat16), got, preferred_element_type=jnp.float32)
    spectrum = spectrum + jnp.dot(low.astype(jnp.bfloat16), got, preferred_element_type=jnp.float32)
    length = forward.shape[0] // 4
    l_re, l_im, g_re, g_im = (spectrum[i * length:(i + 1) * length] for i in range(4))
    z_re = l_re * g_re + l_im * g_im
    z_im = l_im * g_re - l_re * g_im
    z = jnp.concatenate([z_re, z_im])
    return jnp.dot(inverse, z, precision=lax.Precision.HIGH, preferred_element_type=jnp.float32)


def sandwich(left, field, right):
    inner = jnp.matmul(left, field, precision=lax.Precision.HIGH)
    return jnp.matmul(inner, right, precision=lax.Precision.HIGH)


def by_destination(g_lesser, g_greater, groups, tile_width):
    e_local = g_lesser.shape[2]

    def kernel(lesser_ref, greater_ref, out_ref):
        for dest in range(groups):
            for which, ref in enumerate((lesser_ref, greater_ref)):
                for part in range(2):
                    row = (which * 2 + part) * e_local
                    out_ref[dest, row:row + e_local, :] = ref[0, part, :, dest * tile_width:(dest + 1) * tile_width]

    return pl.pallas_call(
        kernel,
        out_shape=jax.ShapeDtypeStruct((groups, 4 * e_local, tile_width), g_lesser.dtype),
        in_specs=[pl.BlockSpec(memory_space=pltpu.VMEM)] * 2,
        out_specs=pl.BlockSpec(memory_space=pltpu.VMEM),
    )(g_lesser, g_greater)


def per_device(g_lesser, g_greater, v_diag, v_couple):
    groups = lax.axis_size("energy")
    e_local = g_lesser.shape[2]
    elements = g_lesser.shape[3]
    count = e_local * groups
    tile_width = (elements + groups * QUANT - 1) // (groups * QUANT) * QUANT
    padding = tile_width * groups - elements

    couple_own = v_couple[0]
    forward, inverse = tables(count, e_local, groups)

    if padding == 0:
        both = by_destination(g_lesser, g_greater, groups, tile_width)
    else:
        both = jnp.stack([g_lesser[0], g_greater[0]])
        both = jnp.pad(both, ((0, 0), (0, 0), (0, 0), (0, padding)))
        both = both.reshape(2, 2, e_local, groups, tile_width)
        both = both.transpose(3, 0, 1, 2, 4).reshape(groups, 4 * e_local, tile_width)
    got = lax.all_to_all(both, "energy", 0, 0, tiled=True)
    polar_tile = correlate(got.reshape(groups * 4 * e_local, tile_width), forward, inverse)

    send = polar_tile.reshape(groups, 2 * e_local, tile_width)
    back = lax.all_to_all(send, "energy", 0, 0, tiled=True)
    back = back.reshape(groups, 2, e_local, tile_width).transpose(1, 2, 0, 3)
    back = back.reshape(2, e_local, groups * tile_width)[:, :, :elements]
    polar = back.reshape(2, e_local, BS, BS)

    diag_block = v_diag[0]
    polar_above = shifted(polar, "space", -1)
    to_next = sandwich(couple_own.T, polar, couple_own)
    from_below = shifted(to_next, "space", 1)
    local = sandwich(diag_block, polar, diag_block)
    from_above = sandwich(couple_own, polar_above, couple_own.T)
    local, from_below, from_above = lax.optimization_barrier((local, from_below, from_above))
    shape = (1, 2, e_local, elements)
    return local.reshape(shape) + from_below.reshape(shape) + from_above.reshape(shape)


def solution(mesh):
    placed = (
        P("space", None, "energy", None),
        P("space", None, "energy", None),
        P("space", None, None),
        P("space", None, None),
    )
    return jax.shard_map(
        per_device,
        mesh=mesh,
        in_specs=placed,
        out_specs=P("space", None, "energy", None),
        check_vma=False,
    )
```

```python
import math

import jax
import jax.numpy as jnp
from jax import lax
from jax.experimental import pallas as pl
from jax.experimental.pallas import tpu as pltpu
from jax.sharding import PartitionSpec as P

BS = 128
QUANT = 128


def shifted(x, axis, by):
    devices = lax.axis_size(axis)
    pairs = [(i, i + by) for i in range(devices) if 0 <= i + by < devices]
    return lax.ppermute(x, axis, pairs)


def tables(count, e_local, groups):
    length = 2 * count
    k = lax.iota(jnp.int32, length)
    n = lax.iota(jnp.int32, count)
    phase = ((k[:, None] * n[None, :]) % length).astype(jnp.float32) * (2.0 * math.pi / length)
    cosine = jnp.cos(phase)
    sine = jnp.sin(phase)
    re_rows = jnp.stack([cosine, sine], axis=1)
    im_rows = jnp.stack([-sine, cosine], axis=1)
    per_part = jnp.stack([re_rows, im_rows])
    per_part = per_part.reshape(2, length, 2, groups, e_local).transpose(0, 1, 3, 2, 4)
    zero = jnp.zeros_like(per_part)
    lesser_rows = jnp.stack([per_part, zero], axis=3)
    greater_rows = jnp.stack([zero, per_part], axis=3)
    forward = jnp.stack([lesser_rows, greater_rows]).reshape(4 * length, 4 * count)
    scale = count ** (-0.5) / length
    inv_cos = cosine.T * scale
    inv_sin = sine.T * scale
    ri0 = jnp.concatenate([-inv_sin, -inv_cos], axis=1)
    ri1 = jnp.concatenate([inv_cos, -inv_sin], axis=1)
    inverse = jnp.stack([ri0, ri1]).reshape(2, groups, e_local, 2 * length)
    inverse = inverse.transpose(1, 0, 2, 3).reshape(2 * count, 2 * length)
    return forward, inverse


def correlate(got, forward, inverse):
    high = lax.reduce_precision(forward, exponent_bits=8, mantissa_bits=7)
    low = forward - high
    spectrum = jnp.dot(high.astype(jnp.bfloat16), got, preferred_element_type=jnp.float32)
    spectrum = spectrum + jnp.dot(low.astype(jnp.bfloat16), got, preferred_element_type=jnp.float32)
    length = forward.shape[0] // 4
    l_re, l_im, g_re, g_im = (spectrum[i * length:(i + 1) * length] for i in range(4))
    z_re = l_re * g_re + l_im * g_im
    z_im = l_im * g_re - l_re * g_im
    z = jnp.concatenate([z_re, z_im])
    return jnp.dot(inverse, z, precision=lax.Precision.HIGH, preferred_element_type=jnp.float32)


def sandwich(left, field, right):
    inner = jnp.matmul(left, field, precision=lax.Precision.HIGH)
    return jnp.matmul(inner, right, precision=lax.Precision.HIGH)


def by_destination(g_lesser, g_greater, groups, tile_width):
    e_local = g_lesser.shape[2]

    def kernel(lesser_ref, greater_ref, out_ref):
        for dest in range(groups):
            for which, ref in enumerate((lesser_ref, greater_ref)):
                for part in range(2):
                    row = (which * 2 + part) * e_local
                    out_ref[dest, row:row + e_local, :] = ref[0, part, :, dest * tile_width:(dest + 1) * tile_width]

    return pl.pallas_call(
        kernel,
        out_shape=jax.ShapeDtypeStruct((groups, 4 * e_local, tile_width), g_lesser.dtype),
        in_specs=[pl.BlockSpec(memory_space=pltpu.VMEM)] * 2,
        out_specs=pl.BlockSpec(memory_space=pltpu.VMEM),
    )(g_lesser, g_greater)


def per_device(g_lesser, g_greater, v_diag, v_couple):
    groups = lax.axis_size("energy")
    e_local = g_lesser.shape[2]
    elements = g_lesser.shape[3]
    count = e_local * groups
    tile_width = (elements + groups * QUANT - 1) // (groups * QUANT) * QUANT
    padding = tile_width * groups - elements

    couple_own = v_couple[0]
    forward, inverse = tables(count, e_local, groups)

    if padding == 0:
        both = by_destination(g_lesser, g_greater, groups, tile_width)
    else:
        both = jnp.stack([g_lesser[0], g_greater[0]])
        both = jnp.pad(both, ((0, 0), (0, 0), (0, 0), (0, padding)))
        both = both.reshape(2, 2, e_local, groups, tile_width)
        both = both.transpose(3, 0, 1, 2, 4).reshape(groups, 4 * e_local, tile_width)
    got = lax.all_to_all(both, "energy", 0, 0, tiled=True)
    polar_tile = correlate(got.reshape(groups * 4 * e_local, tile_width), forward, inverse)

    send = polar_tile.reshape(groups, 2 * e_local, tile_width)
    back = lax.all_to_all(send, "energy", 0, 0, tiled=True)
    back = back.reshape(groups, 2, e_local, tile_width).transpose(1, 2, 0, 3)
    back = back.reshape(2, e_local, groups * tile_width)[:, :, :elements]
    polar = back.reshape(2, e_local, BS, BS)

    diag_block = v_diag[0]
    polar_above = shifted(polar, "space", -1)
    to_next = sandwich(couple_own.T, polar, couple_own)
    from_below = shifted(to_next, "space", 1)
    local = sandwich(diag_block, polar, diag_block)
    from_above = sandwich(couple_own, polar_above, couple_own.T)
    shape = (1, 2, e_local, elements)
    partial = (local + from_above).reshape(shape)
    partial, from_below = lax.optimization_barrier((partial, from_below))
    return partial + from_below.reshape(shape)


def solution(mesh):
    placed = (
        P("space", None, "energy", None),
        P("space", None, "energy", None),
        P("space", None, None),
        P("space", None, None),
    )
    return jax.shard_map(
        per_device,
        mesh=mesh,
        in_specs=placed,
        out_specs=P("space", None, "energy", None),
        check_vma=False,
    )
```

```python
import math

import jax
import jax.numpy as jnp
from jax import lax
from jax.experimental import pallas as pl
from jax.experimental.pallas import tpu as pltpu
from jax.sharding import PartitionSpec as P

BS = 128
QUANT = 128


def shifted(x, axis, by):
    devices = lax.axis_size(axis)
    pairs = [(i, i + by) for i in range(devices) if 0 <= i + by < devices]
    return lax.ppermute(x, axis, pairs)


def tables(count, e_local, groups):
    length = 2 * count
    k = lax.iota(jnp.int32, length)
    n = lax.iota(jnp.int32, count)
    phase = ((k[:, None] * n[None, :]) % length).astype(jnp.float32) * (2.0 * math.pi / length)
    cosine = jnp.cos(phase)
    sine = jnp.sin(phase)
    re_rows = jnp.stack([cosine, sine], axis=1)
    im_rows = jnp.stack([-sine, cosine], axis=1)
    per_part = jnp.stack([re_rows, im_rows])
    per_part = per_part.reshape(2, length, 2, groups, e_local).transpose(0, 1, 3, 2, 4)
    zero = jnp.zeros_like(per_part)
    lesser_rows = jnp.stack([per_part, zero], axis=3)
    greater_rows = jnp.stack([zero, per_part], axis=3)
    forward = jnp.stack([lesser_rows, greater_rows]).reshape(4 * length, 4 * count)
    scale = count ** (-0.5) / length
    inv_cos = cosine.T * scale
    inv_sin = sine.T * scale
    ri0 = jnp.concatenate([-inv_sin, -inv_cos], axis=1)
    ri1 = jnp.concatenate([inv_cos, -inv_sin], axis=1)
    inverse = jnp.stack([ri0, ri1]).reshape(2, groups, e_local, 2 * length)
    inverse = inverse.transpose(1, 0, 2, 3).reshape(2 * count, 2 * length)
    return forward, inverse


def correlate(got, forward, inverse):
    high = lax.reduce_precision(forward, exponent_bits=8, mantissa_bits=7)
    low = forward - high
    spectrum = jnp.dot(high.astype(jnp.bfloat16), got, preferred_element_type=jnp.float32)
    spectrum = spectrum + jnp.dot(low.astype(jnp.bfloat16), got, preferred_element_type=jnp.float32)
    length = forward.shape[0] // 4
    l_re, l_im, g_re, g_im = (spectrum[i * length:(i + 1) * length] for i in range(4))
    z_re = l_re * g_re + l_im * g_im
    z_im = l_im * g_re - l_re * g_im
    z = jnp.concatenate([z_re, z_im])
    return jnp.dot(inverse, z, precision=lax.Precision.HIGH, preferred_element_type=jnp.float32)


def sandwich(left, field, right):
    inner = jnp.matmul(left, field, precision=lax.Precision.HIGH)
    return jnp.matmul(inner, right, precision=lax.Precision.HIGH)


def by_destination(g_lesser, g_greater, groups, tile_width):
    e_local = g_lesser.shape[2]

    def kernel(lesser_hbm, greater_hbm, out_ref, sems):
        copies = []
        for dest in range(groups):
            for which, ref in enumerate((lesser_hbm, greater_hbm)):
                copy = pltpu.make_async_copy(
                    ref.at[0, :, :, pl.ds(dest * tile_width, tile_width)],
                    out_ref.at[dest, pl.ds(2 * which, 2)],
                    sems.at[dest * 2 + which],
                )
                copy.start()
                copies.append(copy)
        for copy in copies:
            copy.wait()

    return pl.pallas_call(
        kernel,
        out_shape=jax.ShapeDtypeStruct((groups, 4, e_local, tile_width), g_lesser.dtype),
        in_specs=[pl.BlockSpec(memory_space=pl.ANY)] * 2,
        out_specs=pl.BlockSpec(memory_space=pltpu.VMEM),
        scratch_shapes=[pltpu.SemaphoreType.DMA((2 * groups,))],
    )(g_lesser, g_greater)


def per_device(g_lesser, g_greater, v_diag, v_couple):
    groups = lax.axis_size("energy")
    e_local = g_lesser.shape[2]
    elements = g_lesser.shape[3]
    count = e_local * groups
    tile_width = (elements + groups * QUANT - 1) // (groups * QUANT) * QUANT
    padding = tile_width * groups - elements

    couple_own = v_couple[0]
    forward, inverse = tables(count, e_local, groups)

    if padding == 0:
        both = by_destination(g_lesser, g_greater, groups, tile_width)
    else:
        both = jnp.stack([g_lesser[0], g_greater[0]])
        both = jnp.pad(both, ((0, 0), (0, 0), (0, 0), (0, padding)))
        both = both.reshape(2, 2, e_local, groups, tile_width)
        both = both.transpose(3, 0, 1, 2, 4).reshape(groups, 4 * e_local, tile_width)
    got = lax.all_to_all(both, "energy", 0, 0, tiled=True)
    polar_tile = correlate(got.reshape(groups * 4 * e_local, tile_width), forward, inverse)

    send = polar_tile.reshape(groups, 2 * e_local, tile_width)
    back = lax.all_to_all(send, "energy", 0, 0, tiled=True)
    back = back.reshape(groups, 2, e_local, tile_width).transpose(1, 2, 0, 3)
    back = back.reshape(2, e_local, groups * tile_width)[:, :, :elements]
    polar = back.reshape(2, e_local, BS, BS)

    diag_block = v_diag[0]
    polar_above = shifted(polar, "space", -1)
    to_next = sandwich(couple_own.T, polar, couple_own)
    from_below = shifted(to_next, "space", 1)
    local = sandwich(diag_block, polar, diag_block)
    from_above = sandwich(couple_own, polar_above, couple_own.T)
    shape = (1, 2, e_local, elements)
    partial = (local + from_above).reshape(shape)
    partial, from_below = lax.optimization_barrier((partial, from_below))
    return partial + from_below.reshape(shape)


def solution(mesh):
    placed = (
        P("space", None, "energy", None),
        P("space", None, "energy", None),
        P("space", None, None),
        P("space", None, None),
    )
    return jax.shard_map(
        per_device,
        mesh=mesh,
        in_specs=placed,
        out_specs=P("space", None, "energy", None),
        check_vma=False,
    )
```

```python
import math

import jax
import jax.numpy as jnp
from jax import lax
from jax.experimental import pallas as pl
from jax.experimental.pallas import tpu as pltpu
from jax.sharding import PartitionSpec as P

BS = 128
QUANT = 128


def shifted(x, axis, by):
    devices = lax.axis_size(axis)
    pairs = [(i, i + by) for i in range(devices) if 0 <= i + by < devices]
    return lax.ppermute(x, axis, pairs)


def tables(count, e_local, groups):
    length = 2 * count
    k = lax.iota(jnp.int32, length)
    n = lax.iota(jnp.int32, count)
    phase = ((k[:, None] * n[None, :]) % length).astype(jnp.float32) * (2.0 * math.pi / length)
    cosine = jnp.cos(phase)
    sine = jnp.sin(phase)
    re_rows = jnp.stack([cosine, sine], axis=1)
    im_rows = jnp.stack([-sine, cosine], axis=1)
    per_part = jnp.stack([re_rows, im_rows])
    per_part = per_part.reshape(2, length, 2, groups, e_local).transpose(0, 1, 3, 2, 4)
    zero = jnp.zeros_like(per_part)
    lesser_rows = jnp.stack([per_part, zero], axis=3)
    greater_rows = jnp.stack([zero, per_part], axis=3)
    forward = jnp.stack([lesser_rows, greater_rows]).reshape(4 * length, 4 * count)
    scale = count ** (-0.5) / length
    inv_cos = cosine.T * scale
    inv_sin = sine.T * scale
    ri0 = jnp.concatenate([-inv_sin, -inv_cos], axis=1)
    ri1 = jnp.concatenate([inv_cos, -inv_sin], axis=1)
    inverse = jnp.stack([ri0, ri1]).reshape(2, groups, e_local, 2 * length)
    inverse = inverse.transpose(1, 0, 2, 3).reshape(2 * count, 2 * length)
    return forward, inverse


def correlate(got, forward, inverse):
    high = lax.reduce_precision(forward, exponent_bits=8, mantissa_bits=7)
    low = forward - high
    spectrum = jnp.dot(high.astype(jnp.bfloat16), got, preferred_element_type=jnp.float32)
    spectrum = spectrum + jnp.dot(low.astype(jnp.bfloat16), got, preferred_element_type=jnp.float32)
    length = forward.shape[0] // 4
    l_re, l_im, g_re, g_im = (spectrum[i * length:(i + 1) * length] for i in range(4))
    z_re = l_re * g_re + l_im * g_im
    z_im = l_im * g_re - l_re * g_im
    z = jnp.concatenate([z_re, z_im])
    return jnp.dot(inverse, z, precision=lax.Precision.HIGH, preferred_element_type=jnp.float32)


def sandwich(left, field, right):
    inner = jnp.matmul(left, field, precision=lax.Precision.HIGH)
    return jnp.matmul(inner, right, precision=lax.Precision.HIGH)


def by_destination(g_lesser, g_greater, groups, tile_width):
    e_local = g_lesser.shape[2]

    def kernel(lesser_hbm, greater_hbm, out_ref, sems):
        copies = []
        for dest in range(groups):
            for which, ref in enumerate((lesser_hbm, greater_hbm)):
                copy = pltpu.make_async_copy(
                    ref.at[0, :, :, pl.ds(dest * tile_width, tile_width)],
                    out_ref.at[dest, pl.ds(2 * which, 2)],
                    sems.at[dest * 2 + which],
                )
                copy.start()
                copies.append(copy)
        for copy in copies:
            copy.wait()

    return pl.pallas_call(
        kernel,
        out_shape=jax.ShapeDtypeStruct((groups, 4, e_local, tile_width), g_lesser.dtype),
        in_specs=[pl.BlockSpec(memory_space=pl.ANY)] * 2,
        out_specs=pl.BlockSpec(memory_space=pltpu.VMEM),
        scratch_shapes=[pltpu.SemaphoreType.DMA((2 * groups,))],
    )(g_lesser, g_greater)


def per_device(g_lesser, g_greater, v_diag, v_couple):
    groups = lax.axis_size("energy")
    e_local = g_lesser.shape[2]
    elements = g_lesser.shape[3]
    count = e_local * groups
    tile_width = (elements + groups * QUANT - 1) // (groups * QUANT) * QUANT
    padding = tile_width * groups - elements

    couple_own = v_couple[0]
    forward, inverse = tables(count, e_local, groups)

    if padding == 0:
        both = by_destination(g_lesser, g_greater, groups, tile_width)
    else:
        both = jnp.stack([g_lesser[0], g_greater[0]])
        both = jnp.pad(both, ((0, 0), (0, 0), (0, 0), (0, padding)))
        both = both.reshape(2, 2, e_local, groups, tile_width)
        both = both.transpose(3, 0, 1, 2, 4).reshape(groups, 4 * e_local, tile_width)
    got = lax.all_to_all(both, "energy", 0, 0, tiled=True)
    polar_tile = correlate(got.reshape(groups * 4 * e_local, tile_width), forward, inverse)

    send = polar_tile.reshape(groups, 2 * e_local, tile_width)
    back = lax.all_to_all(send, "energy", 0, 0, tiled=True)
    back_above = shifted(back, "space", -1)

    def as_blocks(received):
        received = received.reshape(groups, 2, e_local, tile_width).transpose(1, 2, 0, 3)
        received = received.reshape(2, e_local, groups * tile_width)[:, :, :elements]
        return received.reshape(2, e_local, BS, BS)

    polar = as_blocks(back)
    polar_above = as_blocks(back_above)
    diag_block = v_diag[0]
    to_next = sandwich(couple_own.T, polar, couple_own)
    from_below = shifted(to_next, "space", 1)
    local = sandwich(diag_block, polar, diag_block)
    from_above = sandwich(couple_own, polar_above, couple_own.T)
    shape = (1, 2, e_local, elements)
    partial = (local + from_above).reshape(shape)
    partial, from_below = lax.optimization_barrier((partial, from_below))
    return partial + from_below.reshape(shape)


def solution(mesh):
    placed = (
        P("space", None, "energy", None),
        P("space", None, "energy", None),
        P("space", None, None),
        P("space", None, None),
    )
    return jax.shard_map(
        per_device,
        mesh=mesh,
        in_specs=placed,
        out_specs=P("space", None, "energy", None),
        check_vma=False,
    )
```

```python
import math

import jax
import jax.numpy as jnp
from jax import lax
from jax.experimental import pallas as pl
from jax.experimental.pallas import tpu as pltpu
from jax.sharding import PartitionSpec as P

BS = 128
QUANT = 128


def shifted(x, axis, by):
    devices = lax.axis_size(axis)
    pairs = [(i, i + by) for i in range(devices) if 0 <= i + by < devices]
    return lax.ppermute(x, axis, pairs)


def tables(count, e_local, groups):
    length = 2 * count
    k = lax.iota(jnp.int32, length)
    n = lax.iota(jnp.int32, count)
    phase = ((k[:, None] * n[None, :]) % length).astype(jnp.float32) * (2.0 * math.pi / length)
    cosine = jnp.cos(phase)
    sine = jnp.sin(phase)
    re_rows = jnp.stack([cosine, sine], axis=1)
    im_rows = jnp.stack([-sine, cosine], axis=1)
    per_part = jnp.stack([re_rows, im_rows])
    per_part = per_part.reshape(2, length, 2, groups, e_local).transpose(0, 1, 3, 2, 4)
    zero = jnp.zeros_like(per_part)
    lesser_rows = jnp.stack([per_part, zero], axis=3)
    greater_rows = jnp.stack([zero, per_part], axis=3)
    forward = jnp.stack([lesser_rows, greater_rows]).reshape(4 * length, 4 * count)
    scale = count ** (-0.5) / length
    inv_cos = cosine.T * scale
    inv_sin = sine.T * scale
    ri0 = jnp.concatenate([-inv_sin, -inv_cos], axis=1)
    ri1 = jnp.concatenate([inv_cos, -inv_sin], axis=1)
    inverse = jnp.stack([ri0, ri1]).reshape(2, groups, e_local, 2 * length)
    inverse = inverse.transpose(1, 0, 2, 3).reshape(2 * count, 2 * length)
    return forward, inverse


def correlate(got, forward, inverse):
    high = lax.reduce_precision(forward, exponent_bits=8, mantissa_bits=7)
    low = forward - high
    spectrum = jnp.dot(high.astype(jnp.bfloat16), got, preferred_element_type=jnp.float32)
    spectrum = spectrum + jnp.dot(low.astype(jnp.bfloat16), got, preferred_element_type=jnp.float32)
    length = forward.shape[0] // 4
    l_re, l_im, g_re, g_im = (spectrum[i * length:(i + 1) * length] for i in range(4))
    z_re = l_re * g_re + l_im * g_im
    z_im = l_im * g_re - l_re * g_im
    z = jnp.concatenate([z_re, z_im])
    return jnp.dot(inverse, z, precision=lax.Precision.HIGH, preferred_element_type=jnp.float32)


def sandwich(left, field, right):
    inner = jnp.matmul(left, field, precision=lax.Precision.HIGH)
    return jnp.matmul(inner, right, precision=lax.Precision.HIGH)


def by_destination(g_lesser, g_greater, groups, tile_width):
    e_local = g_lesser.shape[2]

    def kernel(lesser_hbm, greater_hbm, out_hbm, sems):
        copies = []
        for dest in range(groups):
            for which, ref in enumerate((lesser_hbm, greater_hbm)):
                copy = pltpu.make_async_copy(
                    ref.at[0, :, :, pl.ds(dest * tile_width, tile_width)],
                    out_hbm.at[dest, pl.ds(2 * which, 2)],
                    sems.at[dest * 2 + which],
                )
                copy.start()
                copies.append(copy)
        for copy in copies:
            copy.wait()

    return pl.pallas_call(
        kernel,
        out_shape=jax.ShapeDtypeStruct((groups, 4, e_local, tile_width), g_lesser.dtype),
        in_specs=[pl.BlockSpec(memory_space=pl.ANY)] * 2,
        out_specs=pl.BlockSpec(memory_space=pl.ANY),
        scratch_shapes=[pltpu.SemaphoreType.DMA((2 * groups,))],
    )(g_lesser, g_greater)


def per_device(g_lesser, g_greater, v_diag, v_couple):
    groups = lax.axis_size("energy")
    e_local = g_lesser.shape[2]
    elements = g_lesser.shape[3]
    count = e_local * groups
    tile_width = (elements + groups * QUANT - 1) // (groups * QUANT) * QUANT
    padding = tile_width * groups - elements

    couple_own = v_couple[0]
    forward, inverse = tables(count, e_local, groups)

    if padding == 0:
        both = by_destination(g_lesser, g_greater, groups, tile_width)
    else:
        both = jnp.stack([g_lesser[0], g_greater[0]])
        both = jnp.pad(both, ((0, 0), (0, 0), (0, 0), (0, padding)))
        both = both.reshape(2, 2, e_local, groups, tile_width)
        both = both.transpose(3, 0, 1, 2, 4).reshape(groups, 4 * e_local, tile_width)
    got = lax.all_to_all(both, "energy", 0, 0, tiled=True)
    polar_tile = correlate(got.reshape(groups * 4 * e_local, tile_width), forward, inverse)

    send = polar_tile.reshape(groups, 2 * e_local, tile_width)
    back = lax.all_to_all(send, "energy", 0, 0, tiled=True)
    back_above = shifted(back, "space", -1)

    def as_blocks(received):
        received = received.reshape(groups, 2, e_local, tile_width).transpose(1, 2, 0, 3)
        received = received.reshape(2, e_local, groups * tile_width)[:, :, :elements]
        return received.reshape(2, e_local, BS, BS)

    polar = as_blocks(back)
    polar_above = as_blocks(back_above)
    diag_block = v_diag[0]
    to_next = sandwich(couple_own.T, polar, couple_own)
    from_below = shifted(to_next, "space", 1)
    local = sandwich(diag_block, polar, diag_block)
    from_above = sandwich(couple_own, polar_above, couple_own.T)
    shape = (1, 2, e_local, elements)
    partial = (local + from_above).reshape(shape)
    partial, from_below = lax.optimization_barrier((partial, from_below))
    return partial + from_below.reshape(shape)


def solution(mesh):
    placed = (
        P("space", None, "energy", None),
        P("space", None, "energy", None),
        P("space", None, None),
        P("space", None, None),
    )
    return jax.shard_map(
        per_device,
        mesh=mesh,
        in_specs=placed,
        out_specs=P("space", None, "energy", None),
        check_vma=False,
    )
```

```python
import math

import jax
import jax.numpy as jnp
from jax import lax
from jax.experimental import pallas as pl
from jax.experimental.pallas import tpu as pltpu
from jax.sharding import PartitionSpec as P

BS = 128
QUANT = 128


def shifted(x, axis, by):
    devices = lax.axis_size(axis)
    pairs = [(i, i + by) for i in range(devices) if 0 <= i + by < devices]
    return lax.ppermute(x, axis, pairs)


def tables(count, e_local, groups):
    length = 2 * count
    k = lax.iota(jnp.int32, length)
    n = lax.iota(jnp.int32, count)
    phase = ((k[:, None] * n[None, :]) % length).astype(jnp.float32) * (2.0 * math.pi / length)
    cosine = jnp.cos(phase)
    sine = jnp.sin(phase)
    re_rows = jnp.stack([cosine, sine], axis=1)
    im_rows = jnp.stack([-sine, cosine], axis=1)
    per_part = jnp.stack([re_rows, im_rows])
    per_part = per_part.reshape(2, length, 2, groups, e_local).transpose(0, 1, 3, 2, 4)
    zero = jnp.zeros_like(per_part)
    lesser_rows = jnp.stack([per_part, zero], axis=3)
    greater_rows = jnp.stack([zero, per_part], axis=3)
    forward = jnp.stack([lesser_rows, greater_rows]).reshape(4 * length, 4 * count)
    scale = count ** (-0.5) / length
    inv_cos = cosine.T * scale
    inv_sin = sine.T * scale
    ri0 = jnp.concatenate([-inv_sin, -inv_cos], axis=1)
    ri1 = jnp.concatenate([inv_cos, -inv_sin], axis=1)
    inverse = jnp.stack([ri0, ri1]).reshape(2, groups, e_local, 2 * length)
    inverse = inverse.transpose(1, 0, 2, 3).reshape(2 * count, 2 * length)
    return forward, inverse


def split_bf16(table):
    high = lax.reduce_precision(table, exponent_bits=8, mantissa_bits=7)
    return high.astype(jnp.bfloat16), (table - high).astype(jnp.bfloat16)


def correlate(got, forward, inverse):
    length = forward.shape[0] // 4
    f_hi, f_lo = split_bf16(forward)
    re_hi, re_lo = split_bf16(inverse[:, :length])
    im_hi, im_lo = split_bf16(inverse[:, length:])

    def kernel(y_ref, f_hi_ref, f_lo_ref, re_hi_ref, re_lo_ref, im_hi_ref, im_lo_ref, o_ref):
        y = y_ref[...]
        spectrum = jnp.dot(f_hi_ref[...], y, preferred_element_type=jnp.float32)
        spectrum = spectrum + jnp.dot(f_lo_ref[...], y, preferred_element_type=jnp.float32)
        l_re, l_im, g_re, g_im = (spectrum[i * length:(i + 1) * length] for i in range(4))
        z_re = l_re * g_re + l_im * g_im
        z_im = l_im * g_re - l_re * g_im
        total = None
        for z, hi_ref, lo_ref in ((z_re, re_hi_ref, re_lo_ref), (z_im, im_hi_ref, im_lo_ref)):
            z_hi = z.astype(jnp.bfloat16)
            z_lo = (z - z_hi.astype(jnp.float32)).astype(jnp.bfloat16)
            hi = hi_ref[...]
            part = jnp.dot(hi, z_hi, preferred_element_type=jnp.float32)
            part = part + jnp.dot(hi, z_lo, preferred_element_type=jnp.float32)
            part = part + jnp.dot(lo_ref[...], z_hi, preferred_element_type=jnp.float32)
            total = part if total is None else total + part
        o_ref[...] = total

    return pl.pallas_call(
        kernel,
        out_shape=jax.ShapeDtypeStruct((inverse.shape[0], got.shape[1]), jnp.float32),
        in_specs=[pl.BlockSpec(memory_space=pltpu.VMEM)] * 7,
        out_specs=pl.BlockSpec(memory_space=pltpu.VMEM),
    )(got, f_hi, f_lo, re_hi, re_lo, im_hi, im_lo)


def sandwich(left, field, right):
    inner = jnp.matmul(left, field, precision=lax.Precision.HIGH)
    return jnp.matmul(inner, right, precision=lax.Precision.HIGH)


def by_destination(g_lesser, g_greater, groups, tile_width):
    e_local = g_lesser.shape[2]

    def kernel(lesser_hbm, greater_hbm, out_ref, sems):
        copies = []
        for dest in range(groups):
            for which, ref in enumerate((lesser_hbm, greater_hbm)):
                copy = pltpu.make_async_copy(
                    ref.at[0, :, :, pl.ds(dest * tile_width, tile_width)],
                    out_ref.at[dest, pl.ds(2 * which, 2)],
                    sems.at[dest * 2 + which],
                )
                copy.start()
                copies.append(copy)
        for copy in copies:
            copy.wait()

    return pl.pallas_call(
        kernel,
        out_shape=jax.ShapeDtypeStruct((groups, 4, e_local, tile_width), g_lesser.dtype),
        in_specs=[pl.BlockSpec(memory_space=pl.ANY)] * 2,
        out_specs=pl.BlockSpec(memory_space=pltpu.VMEM),
        scratch_shapes=[pltpu.SemaphoreType.DMA((2 * groups,))],
    )(g_lesser, g_greater)


def per_device(g_lesser, g_greater, v_diag, v_couple):
    groups = lax.axis_size("energy")
    e_local = g_lesser.shape[2]
    elements = g_lesser.shape[3]
    count = e_local * groups
    tile_width = (elements + groups * QUANT - 1) // (groups * QUANT) * QUANT
    padding = tile_width * groups - elements

    couple_own = v_couple[0]
    forward, inverse = tables(count, e_local, groups)

    if padding == 0:
        both = by_destination(g_lesser, g_greater, groups, tile_width)
    else:
        both = jnp.stack([g_lesser[0], g_greater[0]])
        both = jnp.pad(both, ((0, 0), (0, 0), (0, 0), (0, padding)))
        both = both.reshape(2, 2, e_local, groups, tile_width)
        both = both.transpose(3, 0, 1, 2, 4).reshape(groups, 4 * e_local, tile_width)
    got = lax.all_to_all(both, "energy", 0, 0, tiled=True)
    polar_tile = correlate(got.reshape(groups * 4 * e_local, tile_width), forward, inverse)

    send = polar_tile.reshape(groups, 2 * e_local, tile_width)
    back = lax.all_to_all(send, "energy", 0, 0, tiled=True)
    back_above = shifted(back, "space", -1)

    def as_blocks(received):
        received = received.reshape(groups, 2, e_local, tile_width).transpose(1, 2, 0, 3)
        received = received.reshape(2, e_local, groups * tile_width)[:, :, :elements]
        return received.reshape(2, e_local, BS, BS)

    polar = as_blocks(back)
    polar_above = as_blocks(back_above)
    diag_block = v_diag[0]
    to_next = sandwich(couple_own.T, polar, couple_own)
    from_below = shifted(to_next, "space", 1)
    local = sandwich(diag_block, polar, diag_block)
    from_above = sandwich(couple_own, polar_above, couple_own.T)
    shape = (1, 2, e_local, elements)
    partial = (local + from_above).reshape(shape)
    partial, from_below = lax.optimization_barrier((partial, from_below))
    return partial + from_below.reshape(shape)


def solution(mesh):
    placed = (
        P("space", None, "energy", None),
        P("space", None, "energy", None),
        P("space", None, None),
        P("space", None, None),
    )
    return jax.shard_map(
        per_device,
        mesh=mesh,
        in_specs=placed,
        out_specs=P("space", None, "energy", None),
        check_vma=False,
    )
```

```python
import math

import jax
import jax.numpy as jnp
from jax import lax
from jax.experimental import pallas as pl
from jax.experimental.pallas import tpu as pltpu
from jax.sharding import PartitionSpec as P

BS = 128
QUANT = 128


def shifted(x, axis, by):
    devices = lax.axis_size(axis)
    pairs = [(i, i + by) for i in range(devices) if 0 <= i + by < devices]
    return lax.ppermute(x, axis, pairs)


def tables(count, e_local, groups):
    length = 2 * count
    k = lax.iota(jnp.int32, length)
    n = lax.iota(jnp.int32, count)
    phase = ((k[:, None] * n[None, :]) % length).astype(jnp.float32) * (2.0 * math.pi / length)
    cosine = jnp.cos(phase)
    sine = jnp.sin(phase)
    re_rows = jnp.stack([cosine, sine], axis=1)
    im_rows = jnp.stack([-sine, cosine], axis=1)
    per_part = jnp.stack([re_rows, im_rows])
    per_part = per_part.reshape(2, length, 2, groups, e_local).transpose(0, 1, 3, 2, 4)
    zero = jnp.zeros_like(per_part)
    lesser_rows = jnp.stack([per_part, zero], axis=3)
    greater_rows = jnp.stack([zero, per_part], axis=3)
    forward = jnp.stack([lesser_rows, greater_rows]).reshape(4 * length, 4 * count)
    scale = count ** (-0.5) / length
    inv_cos = cosine.T * scale
    inv_sin = sine.T * scale
    ri0 = jnp.concatenate([-inv_sin, -inv_cos], axis=1)
    ri1 = jnp.concatenate([inv_cos, -inv_sin], axis=1)
    inverse = jnp.stack([ri0, ri1]).reshape(2, groups, e_local, 2 * length)
    inverse = inverse.transpose(1, 0, 2, 3).reshape(2 * count, 2 * length)
    return forward, inverse


def correlate(got, forward, inverse):
    high = lax.reduce_precision(forward, exponent_bits=8, mantissa_bits=7)
    low = forward - high
    spectrum = jnp.dot(high.astype(jnp.bfloat16), got, preferred_element_type=jnp.float32)
    spectrum = spectrum + jnp.dot(low.astype(jnp.bfloat16), got, preferred_element_type=jnp.float32)
    length = forward.shape[0] // 4
    l_re, l_im, g_re, g_im = (spectrum[i * length:(i + 1) * length] for i in range(4))
    z_re = l_re * g_re + l_im * g_im
    z_im = l_im * g_re - l_re * g_im
    z = jnp.concatenate([z_re, z_im])
    return jnp.dot(inverse, z, precision=lax.Precision.HIGH, preferred_element_type=jnp.float32)


def sandwich(left, field, right):
    inner = jnp.matmul(left, field, precision=lax.Precision.HIGH)
    return jnp.matmul(inner, right, precision=lax.Precision.HIGH)


def by_destination(g_lesser, g_greater, groups, tile_width):
    e_local = g_lesser.shape[2]

    def kernel(lesser_hbm, greater_hbm, out_ref, sems):
        copies = []
        for dest in range(groups):
            for which, ref in enumerate((lesser_hbm, greater_hbm)):
                copy = pltpu.make_async_copy(
                    ref.at[0, :, :, pl.ds(dest * tile_width, tile_width)],
                    out_ref.at[dest, pl.ds(2 * which, 2)],
                    sems.at[dest * 2 + which],
                )
                copy.start()
                copies.append(copy)
        for copy in copies:
            copy.wait()

    return pl.pallas_call(
        kernel,
        out_shape=jax.ShapeDtypeStruct((groups, 4, e_local, tile_width), g_lesser.dtype),
        in_specs=[pl.BlockSpec(memory_space=pl.ANY)] * 2,
        out_specs=pl.BlockSpec(memory_space=pltpu.VMEM),
        scratch_shapes=[pltpu.SemaphoreType.DMA((2 * groups,))],
    )(g_lesser, g_greater)


def per_device(g_lesser, g_greater, v_diag, v_couple):
    groups = lax.axis_size("energy")
    e_local = g_lesser.shape[2]
    elements = g_lesser.shape[3]
    count = e_local * groups
    tile_width = (elements + groups * QUANT - 1) // (groups * QUANT) * QUANT
    padding = tile_width * groups - elements

    couple_own = v_couple[0]
    forward, inverse = tables(count, e_local, groups)

    if padding == 0:
        both = by_destination(g_lesser, g_greater, groups, tile_width)
    else:
        both = jnp.stack([g_lesser[0], g_greater[0]])
        both = jnp.pad(both, ((0, 0), (0, 0), (0, 0), (0, padding)))
        both = both.reshape(2, 2, e_local, groups, tile_width)
        both = both.transpose(3, 0, 1, 2, 4).reshape(groups, 4 * e_local, tile_width)
    got = lax.all_to_all(both, "energy", 0, 0, tiled=True)
    polar_tile = correlate(got.reshape(groups * 4 * e_local, tile_width), forward, inverse)

    send = polar_tile.reshape(groups, 2 * e_local, tile_width)
    back = lax.all_to_all(send, "energy", 0, 0, tiled=True)
    back_above = shifted(back, "space", -1)

    def as_blocks(received):
        received = received.reshape(groups, 2, e_local, tile_width).transpose(1, 2, 0, 3)
        received = received.reshape(2, e_local, groups * tile_width)[:, :, :elements]
        return received.reshape(2, e_local, BS, BS)

    polar = as_blocks(back)
    polar_above = as_blocks(back_above)
    diag_block = v_diag[0]
    lefts = jnp.stack([couple_own.T, diag_block])
    inner = jnp.einsum("sij,abjk->sabik", lefts, polar, precision=lax.Precision.HIGH)
    to_next = jnp.matmul(inner[0], couple_own, precision=lax.Precision.HIGH)
    from_below = shifted(to_next, "space", 1)
    local = jnp.matmul(inner[1], diag_block, precision=lax.Precision.HIGH)
    from_above = sandwich(couple_own, polar_above, couple_own.T)
    shape = (1, 2, e_local, elements)
    partial = (local + from_above).reshape(shape)
    partial, from_below = lax.optimization_barrier((partial, from_below))
    return partial + from_below.reshape(shape)


def solution(mesh):
    placed = (
        P("space", None, "energy", None),
        P("space", None, "energy", None),
        P("space", None, None),
        P("space", None, None),
    )
    return jax.shard_map(
        per_device,
        mesh=mesh,
        in_specs=placed,
        out_specs=P("space", None, "energy", None),
        check_vma=False,
    )
```

```python
import math

import jax
import jax.numpy as jnp
from jax import lax
from jax.experimental import pallas as pl
from jax.experimental.pallas import tpu as pltpu
from jax.sharding import PartitionSpec as P

BS = 128
QUANT = 128


def shifted(x, axis, by):
    devices = lax.axis_size(axis)
    pairs = [(i, i + by) for i in range(devices) if 0 <= i + by < devices]
    return lax.ppermute(x, axis, pairs)


def tables(count, e_local, groups):
    length = 2 * count
    k = lax.iota(jnp.int32, length)
    n = lax.iota(jnp.int32, count)
    phase = ((k[:, None] * n[None, :]) % length).astype(jnp.float32) * (2.0 * math.pi / length)
    cosine = jnp.cos(phase)
    sine = jnp.sin(phase)
    re_rows = jnp.stack([cosine, sine], axis=1)
    im_rows = jnp.stack([-sine, cosine], axis=1)
    per_part = jnp.stack([re_rows, im_rows])
    per_part = per_part.reshape(2, length, 2, groups, e_local).transpose(0, 1, 3, 2, 4)
    zero = jnp.zeros_like(per_part)
    lesser_rows = jnp.stack([per_part, zero], axis=3)
    greater_rows = jnp.stack([zero, per_part], axis=3)
    forward = jnp.stack([lesser_rows, greater_rows]).reshape(4 * length, 4 * count)
    scale = count ** (-0.5) / length
    inv_cos = cosine.T * scale
    inv_sin = sine.T * scale
    ri0 = jnp.concatenate([-inv_sin, -inv_cos], axis=1)
    ri1 = jnp.concatenate([inv_cos, -inv_sin], axis=1)
    inverse = jnp.stack([ri0, ri1]).reshape(2, groups, e_local, 2 * length)
    inverse = inverse.transpose(1, 0, 2, 3).reshape(2 * count, 2 * length)
    return forward, inverse


def correlate(got, forward, inverse):
    high = lax.reduce_precision(forward, exponent_bits=8, mantissa_bits=7)
    low = forward - high
    spectrum = jnp.dot(high.astype(jnp.bfloat16), got, preferred_element_type=jnp.float32)
    spectrum = spectrum + jnp.dot(low.astype(jnp.bfloat16), got, preferred_element_type=jnp.float32)
    length = forward.shape[0] // 4
    l_re, l_im, g_re, g_im = (spectrum[i * length:(i + 1) * length] for i in range(4))
    z_re = l_re * g_re + l_im * g_im
    z_im = l_im * g_re - l_re * g_im
    z = jnp.concatenate([z_re, z_im])
    return jnp.dot(inverse, z, precision=lax.Precision.HIGH, preferred_element_type=jnp.float32)


def sandwich(left, field, right):
    inner = jnp.matmul(left, field, precision=lax.Precision.HIGH)
    return jnp.matmul(inner, right, precision=lax.Precision.HIGH)


def by_destination(g_lesser, g_greater, groups, tile_width):
    e_local = g_lesser.shape[2]

    def kernel(lesser_hbm, greater_hbm, out_ref, sems):
        copies = []
        for dest in range(groups):
            for which, ref in enumerate((lesser_hbm, greater_hbm)):
                copy = pltpu.make_async_copy(
                    ref.at[0, :, :, pl.ds(dest * tile_width, tile_width)],
                    out_ref.at[dest, pl.ds(2 * which, 2)],
                    sems.at[dest * 2 + which],
                )
                copy.start()
                copies.append(copy)
        for copy in copies:
            copy.wait()

    return pl.pallas_call(
        kernel,
        out_shape=jax.ShapeDtypeStruct((groups, 4, e_local, tile_width), g_lesser.dtype),
        in_specs=[pl.BlockSpec(memory_space=pl.ANY)] * 2,
        out_specs=pl.BlockSpec(memory_space=pltpu.VMEM),
        scratch_shapes=[pltpu.SemaphoreType.DMA((2 * groups,))],
    )(g_lesser, g_greater)


def per_device(g_lesser, g_greater, v_diag, v_couple):
    groups = lax.axis_size("energy")
    e_local = g_lesser.shape[2]
    elements = g_lesser.shape[3]
    count = e_local * groups
    tile_width = (elements + groups * QUANT - 1) // (groups * QUANT) * QUANT
    padding = tile_width * groups - elements

    couple_own = v_couple[0]
    forward, inverse = tables(count, e_local, groups)

    if padding == 0:
        both = by_destination(g_lesser, g_greater, groups, tile_width)
    else:
        both = jnp.stack([g_lesser[0], g_greater[0]])
        both = jnp.pad(both, ((0, 0), (0, 0), (0, 0), (0, padding)))
        both = both.reshape(2, 2, e_local, groups, tile_width)
        both = both.transpose(3, 0, 1, 2, 4).reshape(groups, 4 * e_local, tile_width)
    lefts = jnp.stack([couple_own.T, v_diag[0]])
    both, lefts, couple_own = lax.optimization_barrier((both, lefts, couple_own))
    got = lax.all_to_all(both, "energy", 0, 0, tiled=True)
    polar_tile = correlate(got.reshape(groups * 4 * e_local, tile_width), forward, inverse)

    send = polar_tile.reshape(groups, 2 * e_local, tile_width)
    back = lax.all_to_all(send, "energy", 0, 0, tiled=True)
    back_above = shifted(back, "space", -1)

    def as_blocks(received):
        received = received.reshape(groups, 2, e_local, tile_width).transpose(1, 2, 0, 3)
        received = received.reshape(2, e_local, groups * tile_width)[:, :, :elements]
        return received.reshape(2, e_local, BS, BS)

    polar = as_blocks(back)
    polar_above = as_blocks(back_above)
    diag_block = v_diag[0]
    inner = jnp.einsum("sij,abjk->sabik", lefts, polar, precision=lax.Precision.HIGH)
    to_next = jnp.matmul(inner[0], couple_own, precision=lax.Precision.HIGH)
    from_below = shifted(to_next, "space", 1)
    local = jnp.matmul(inner[1], diag_block, precision=lax.Precision.HIGH)
    from_above = sandwich(couple_own, polar_above, couple_own.T)
    shape = (1, 2, e_local, elements)
    partial = (local + from_above).reshape(shape)
    partial, from_below = lax.optimization_barrier((partial, from_below))
    return partial + from_below.reshape(shape)


def solution(mesh):
    placed = (
        P("space", None, "energy", None),
        P("space", None, "energy", None),
        P("space", None, None),
        P("space", None, None),
    )
    return jax.shard_map(
        per_device,
        mesh=mesh,
        in_specs=placed,
        out_specs=P("space", None, "energy", None),
        check_vma=False,
    )
```

```python
import math

import jax
import jax.numpy as jnp
from jax import lax
from jax.experimental import pallas as pl
from jax.experimental.pallas import tpu as pltpu
from jax.sharding import PartitionSpec as P

BS = 128
QUANT = 128


def shifted(x, axis, by):
    devices = lax.axis_size(axis)
    pairs = [(i, i + by) for i in range(devices) if 0 <= i + by < devices]
    return lax.ppermute(x, axis, pairs)


def tables(count, e_local, groups):
    length = 2 * count
    k = lax.iota(jnp.int32, length)
    n = lax.iota(jnp.int32, count)
    phase = ((k[:, None] * n[None, :]) % length).astype(jnp.float32) * (2.0 * math.pi / length)
    cosine = jnp.cos(phase)
    sine = jnp.sin(phase)
    re_rows = jnp.stack([cosine, sine], axis=1)
    im_rows = jnp.stack([-sine, cosine], axis=1)
    per_part = jnp.stack([re_rows, im_rows])
    per_part = per_part.reshape(2, length, 2, groups, e_local).transpose(0, 1, 3, 2, 4)
    zero = jnp.zeros_like(per_part)
    lesser_rows = jnp.stack([per_part, zero], axis=3)
    greater_rows = jnp.stack([zero, per_part], axis=3)
    forward = jnp.stack([lesser_rows, greater_rows]).reshape(4 * length, 4 * count)
    scale = count ** (-0.5) / length
    inv_cos = cosine.T * scale
    inv_sin = sine.T * scale
    ri0 = jnp.concatenate([-inv_sin, -inv_cos], axis=1)
    ri1 = jnp.concatenate([inv_cos, -inv_sin], axis=1)
    inverse = jnp.stack([ri0, ri1]).reshape(2, groups, e_local, 2 * length)
    inverse = inverse.transpose(1, 0, 2, 3).reshape(2 * count, 2 * length)
    return forward, inverse


def correlate(got, forward, inverse):
    high = lax.reduce_precision(forward, exponent_bits=8, mantissa_bits=7)
    low = forward - high
    split = jnp.concatenate([high, low], axis=1).astype(jnp.bfloat16)
    spectrum = jnp.dot(split, jnp.concatenate([got, got]), preferred_element_type=jnp.float32)
    length = forward.shape[0] // 4
    l_re, l_im, g_re, g_im = (spectrum[i * length:(i + 1) * length] for i in range(4))
    z_re = l_re * g_re + l_im * g_im
    z_im = l_im * g_re - l_re * g_im
    z = jnp.concatenate([z_re, z_im])
    return jnp.dot(inverse, z, precision=lax.Precision.HIGH, preferred_element_type=jnp.float32)


def sandwich(left, field, right):
    inner = jnp.matmul(left, field, precision=lax.Precision.HIGH)
    return jnp.matmul(inner, right, precision=lax.Precision.HIGH)


def by_destination(g_lesser, g_greater, groups, tile_width):
    e_local = g_lesser.shape[2]

    def kernel(lesser_hbm, greater_hbm, out_ref, sems):
        copies = []
        for dest in range(groups):
            for which, ref in enumerate((lesser_hbm, greater_hbm)):
                copy = pltpu.make_async_copy(
                    ref.at[0, :, :, pl.ds(dest * tile_width, tile_width)],
                    out_ref.at[dest, pl.ds(2 * which, 2)],
                    sems.at[dest * 2 + which],
                )
                copy.start()
                copies.append(copy)
        for copy in copies:
            copy.wait()

    return pl.pallas_call(
        kernel,
        out_shape=jax.ShapeDtypeStruct((groups, 4, e_local, tile_width), g_lesser.dtype),
        in_specs=[pl.BlockSpec(memory_space=pl.ANY)] * 2,
        out_specs=pl.BlockSpec(memory_space=pltpu.VMEM),
        scratch_shapes=[pltpu.SemaphoreType.DMA((2 * groups,))],
    )(g_lesser, g_greater)


def per_device(g_lesser, g_greater, v_diag, v_couple):
    groups = lax.axis_size("energy")
    e_local = g_lesser.shape[2]
    elements = g_lesser.shape[3]
    count = e_local * groups
    tile_width = (elements + groups * QUANT - 1) // (groups * QUANT) * QUANT
    padding = tile_width * groups - elements

    couple_own = v_couple[0]
    forward, inverse = tables(count, e_local, groups)

    if padding == 0:
        both = by_destination(g_lesser, g_greater, groups, tile_width)
    else:
        both = jnp.stack([g_lesser[0], g_greater[0]])
        both = jnp.pad(both, ((0, 0), (0, 0), (0, 0), (0, padding)))
        both = both.reshape(2, 2, e_local, groups, tile_width)
        both = both.transpose(3, 0, 1, 2, 4).reshape(groups, 4 * e_local, tile_width)
    got = lax.all_to_all(both, "energy", 0, 0, tiled=True)
    polar_tile = correlate(got.reshape(groups * 4 * e_local, tile_width), forward, inverse)

    send = polar_tile.reshape(groups, 2 * e_local, tile_width)
    back = lax.all_to_all(send, "energy", 0, 0, tiled=True)
    back_above = shifted(back, "space", -1)

    def as_blocks(received):
        received = received.reshape(groups, 2, e_local, tile_width).transpose(1, 2, 0, 3)
        received = received.reshape(2, e_local, groups * tile_width)[:, :, :elements]
        return received.reshape(2, e_local, BS, BS)

    polar = as_blocks(back)
    polar_above = as_blocks(back_above)
    diag_block = v_diag[0]
    to_next = sandwich(couple_own.T, polar, couple_own)
    from_below = shifted(to_next, "space", 1)
    local = sandwich(diag_block, polar, diag_block)
    from_above = sandwich(couple_own, polar_above, couple_own.T)
    shape = (1, 2, e_local, elements)
    partial = (local + from_above).reshape(shape)
    partial, from_below = lax.optimization_barrier((partial, from_below))
    return partial + from_below.reshape(shape)


def solution(mesh):
    placed = (
        P("space", None, "energy", None),
        P("space", None, "energy", None),
        P("space", None, None),
        P("space", None, None),
    )
    return jax.shard_map(
        per_device,
        mesh=mesh,
        in_specs=placed,
        out_specs=P("space", None, "energy", None),
        check_vma=False,
    )
```

```python
import math

import jax
import numpy as np
import jax.numpy as jnp
from jax import lax
from jax.experimental import pallas as pl
from jax.experimental.pallas import tpu as pltpu
from jax.sharding import PartitionSpec as P

BS = 128
QUANT = 128


def shifted(x, axis, by):
    devices = lax.axis_size(axis)
    pairs = [(i, i + by) for i in range(devices) if 0 <= i + by < devices]
    return lax.ppermute(x, axis, pairs)


def tables_np(count, e_local, groups):
    length = 2 * count
    k = np.arange(length, dtype=np.int32)
    n = np.arange(count, dtype=np.int32)
    phase = ((k[:, None] * n[None, :]) % length).astype(np.float32) * np.float32(2.0 * math.pi / length)
    cosine = np.cos(phase)
    sine = np.sin(phase)
    re_rows = np.stack([cosine, sine], axis=1)
    im_rows = np.stack([-sine, cosine], axis=1)
    per_part = np.stack([re_rows, im_rows])
    per_part = per_part.reshape(2, length, 2, groups, e_local).transpose(0, 1, 3, 2, 4)
    zero = np.zeros_like(per_part)
    lesser_rows = np.stack([per_part, zero], axis=3)
    greater_rows = np.stack([zero, per_part], axis=3)
    forward = np.stack([lesser_rows, greater_rows]).reshape(4 * length, 4 * count)
    scale = np.float32(count ** (-0.5) / length)
    inv_cos = cosine.T * scale
    inv_sin = sine.T * scale
    ri0 = np.concatenate([-inv_sin, -inv_cos], axis=1)
    ri1 = np.concatenate([inv_cos, -inv_sin], axis=1)
    inverse = np.stack([ri0, ri1]).reshape(2, groups, e_local, 2 * length)
    inverse = inverse.transpose(1, 0, 2, 3).reshape(2 * count, 2 * length)
    return forward, inverse


def tables(count, e_local, groups):
    length = 2 * count
    k = lax.iota(jnp.int32, length)
    n = lax.iota(jnp.int32, count)
    phase = ((k[:, None] * n[None, :]) % length).astype(jnp.float32) * (2.0 * math.pi / length)
    cosine = jnp.cos(phase)
    sine = jnp.sin(phase)
    re_rows = jnp.stack([cosine, sine], axis=1)
    im_rows = jnp.stack([-sine, cosine], axis=1)
    per_part = jnp.stack([re_rows, im_rows])
    per_part = per_part.reshape(2, length, 2, groups, e_local).transpose(0, 1, 3, 2, 4)
    zero = jnp.zeros_like(per_part)
    lesser_rows = jnp.stack([per_part, zero], axis=3)
    greater_rows = jnp.stack([zero, per_part], axis=3)
    forward = jnp.stack([lesser_rows, greater_rows]).reshape(4 * length, 4 * count)
    scale = count ** (-0.5) / length
    inv_cos = cosine.T * scale
    inv_sin = sine.T * scale
    ri0 = jnp.concatenate([-inv_sin, -inv_cos], axis=1)
    ri1 = jnp.concatenate([inv_cos, -inv_sin], axis=1)
    inverse = jnp.stack([ri0, ri1]).reshape(2, groups, e_local, 2 * length)
    inverse = inverse.transpose(1, 0, 2, 3).reshape(2 * count, 2 * length)
    return forward, inverse


def correlate(got, forward, inverse):
    high = lax.reduce_precision(forward, exponent_bits=8, mantissa_bits=7)
    low = forward - high
    split = jnp.concatenate([high, low], axis=1).astype(jnp.bfloat16)
    spectrum = jnp.dot(split, jnp.concatenate([got, got]), preferred_element_type=jnp.float32)
    length = forward.shape[0] // 4
    l_re, l_im, g_re, g_im = (spectrum[i * length:(i + 1) * length] for i in range(4))
    z_re = l_re * g_re + l_im * g_im
    z_im = l_im * g_re - l_re * g_im
    z = jnp.concatenate([z_re, z_im])
    return jnp.dot(inverse, z, precision=lax.Precision.HIGH, preferred_element_type=jnp.float32)


def sandwich(left, field, right):
    inner = jnp.matmul(left, field, precision=lax.Precision.HIGH)
    return jnp.matmul(inner, right, precision=lax.Precision.HIGH)


def by_destination(g_lesser, g_greater, groups, tile_width):
    e_local = g_lesser.shape[2]

    def kernel(lesser_hbm, greater_hbm, out_ref, sems):
        copies = []
        for dest in range(groups):
            for which, ref in enumerate((lesser_hbm, greater_hbm)):
                copy = pltpu.make_async_copy(
                    ref.at[0, :, :, pl.ds(dest * tile_width, tile_width)],
                    out_ref.at[dest, pl.ds(2 * which, 2)],
                    sems.at[dest * 2 + which],
                )
                copy.start()
                copies.append(copy)
        for copy in copies:
            copy.wait()

    return pl.pallas_call(
        kernel,
        out_shape=jax.ShapeDtypeStruct((groups, 4, e_local, tile_width), g_lesser.dtype),
        in_specs=[pl.BlockSpec(memory_space=pl.ANY)] * 2,
        out_specs=pl.BlockSpec(memory_space=pltpu.VMEM),
        scratch_shapes=[pltpu.SemaphoreType.DMA((2 * groups,))],
    )(g_lesser, g_greater)


def per_device(g_lesser, g_greater, v_diag, v_couple):
    groups = lax.axis_size("energy")
    e_local = g_lesser.shape[2]
    elements = g_lesser.shape[3]
    count = e_local * groups
    tile_width = (elements + groups * QUANT - 1) // (groups * QUANT) * QUANT
    padding = tile_width * groups - elements

    couple_own = v_couple[0]
    make_tables = tables_np if count <= 64 else tables
    forward, inverse = make_tables(count, e_local, groups)

    if padding == 0:
        both = by_destination(g_lesser, g_greater, groups, tile_width)
    else:
        both = jnp.stack([g_lesser[0], g_greater[0]])
        both = jnp.pad(both, ((0, 0), (0, 0), (0, 0), (0, padding)))
        both = both.reshape(2, 2, e_local, groups, tile_width)
        both = both.transpose(3, 0, 1, 2, 4).reshape(groups, 4 * e_local, tile_width)
    got = lax.all_to_all(both, "energy", 0, 0, tiled=True)
    polar_tile = correlate(got.reshape(groups * 4 * e_local, tile_width), forward, inverse)

    send = polar_tile.reshape(groups, 2 * e_local, tile_width)
    back = lax.all_to_all(send, "energy", 0, 0, tiled=True)
    back_above = shifted(back, "space", -1)

    def as_blocks(received):
        received = received.reshape(groups, 2, e_local, tile_width).transpose(1, 2, 0, 3)
        received = received.reshape(2, e_local, groups * tile_width)[:, :, :elements]
        return received.reshape(2, e_local, BS, BS)

    polar = as_blocks(back)
    polar_above = as_blocks(back_above)
    diag_block = v_diag[0]
    to_next = sandwich(couple_own.T, polar, couple_own)
    from_below = shifted(to_next, "space", 1)
    local = sandwich(diag_block, polar, diag_block)
    from_above = sandwich(couple_own, polar_above, couple_own.T)
    shape = (1, 2, e_local, elements)
    partial = (local + from_above).reshape(shape)
    partial, from_below = lax.optimization_barrier((partial, from_below))
    return partial + from_below.reshape(shape)


def solution(mesh):
    placed = (
        P("space", None, "energy", None),
        P("space", None, "energy", None),
        P("space", None, None),
        P("space", None, None),
    )
    return jax.shard_map(
        per_device,
        mesh=mesh,
        in_specs=placed,
        out_specs=P("space", None, "energy", None),
        check_vma=False,
    )
```

```python
import math

import jax
import jax.numpy as jnp
from jax import lax
from jax.experimental import pallas as pl
from jax.experimental.pallas import tpu as pltpu
from jax.sharding import PartitionSpec as P

BS = 128
QUANT = 128


def shifted(x, axis, by):
    devices = lax.axis_size(axis)
    pairs = [(i, i + by) for i in range(devices) if 0 <= i + by < devices]
    return lax.ppermute(x, axis, pairs)


def tables(count, e_local, groups):
    length = 2 * count
    k = lax.iota(jnp.int32, length)
    n = lax.iota(jnp.int32, count)
    phase = ((k[:, None] * n[None, :]) % length).astype(jnp.float32) * (2.0 * math.pi / length)
    cosine = jnp.cos(phase)
    sine = jnp.sin(phase)
    re_rows = jnp.stack([cosine, sine], axis=1)
    im_rows = jnp.stack([-sine, cosine], axis=1)
    per_part = jnp.stack([re_rows, im_rows])
    per_part = per_part.reshape(2, length, 2, groups, e_local).transpose(0, 1, 3, 2, 4)
    zero = jnp.zeros_like(per_part)
    lesser_rows = jnp.stack([per_part, zero], axis=3)
    greater_rows = jnp.stack([zero, per_part], axis=3)
    forward = jnp.stack([lesser_rows, greater_rows]).reshape(4 * length, 4 * count)
    scale = count ** (-0.5) / length
    inv_cos = cosine.T * scale
    inv_sin = sine.T * scale
    ri0 = jnp.concatenate([-inv_sin, -inv_cos], axis=1)
    ri1 = jnp.concatenate([inv_cos, -inv_sin], axis=1)
    inverse = jnp.stack([ri0, ri1]).reshape(2, groups, e_local, 2 * length)
    inverse = inverse.transpose(1, 0, 2, 3).reshape(2 * count, 2 * length)
    return forward, inverse


def correlate(got, forward, inverse):
    high = lax.reduce_precision(forward, exponent_bits=8, mantissa_bits=7)
    low = forward - high
    split = jnp.concatenate([high, low], axis=1).astype(jnp.bfloat16)
    spectrum = jnp.dot(split, jnp.concatenate([got, got]), preferred_element_type=jnp.float32)
    length = forward.shape[0] // 4
    l_re, l_im, g_re, g_im = (spectrum[i * length:(i + 1) * length] for i in range(4))
    z_re = l_re * g_re + l_im * g_im
    z_im = l_im * g_re - l_re * g_im
    z = jnp.concatenate([z_re, z_im])
    return jnp.dot(inverse, z, precision=lax.Precision.HIGH, preferred_element_type=jnp.float32)


def sandwich(left, field, right):
    inner = jnp.matmul(left, field, precision=lax.Precision.HIGH)
    return jnp.matmul(inner, right, precision=lax.Precision.HIGH)


def by_destination(g_lesser, g_greater, groups, tile_width):
    e_local = g_lesser.shape[2]

    def kernel(lesser_hbm, greater_hbm, out_ref, sems):
        copies = []
        for dest in range(groups):
            for which, ref in enumerate((lesser_hbm, greater_hbm)):
                copy = pltpu.make_async_copy(
                    ref.at[0, :, :, pl.ds(dest * tile_width, tile_width)],
                    out_ref.at[dest, pl.ds(2 * which, 2)],
                    sems.at[dest * 2 + which],
                )
                copy.start()
                copies.append(copy)
        for copy in copies:
            copy.wait()

    return pl.pallas_call(
        kernel,
        out_shape=jax.ShapeDtypeStruct((groups, 4, e_local, tile_width), g_lesser.dtype),
        in_specs=[pl.BlockSpec(memory_space=pl.ANY)] * 2,
        out_specs=pl.BlockSpec(memory_space=pltpu.VMEM),
        scratch_shapes=[pltpu.SemaphoreType.DMA((2 * groups,))],
    )(g_lesser, g_greater)


def per_device(g_lesser, g_greater, v_diag, v_couple):
    groups = lax.axis_size("energy")
    e_local = g_lesser.shape[2]
    elements = g_lesser.shape[3]
    count = e_local * groups
    tile_width = (elements + groups * QUANT - 1) // (groups * QUANT) * QUANT
    padding = tile_width * groups - elements

    couple_own = v_couple[0]
    forward, inverse = tables(count, e_local, groups)

    if padding == 0:
        both = by_destination(g_lesser, g_greater, groups, tile_width)
    else:
        both = jnp.stack([g_lesser[0], g_greater[0]])
        both = jnp.pad(both, ((0, 0), (0, 0), (0, 0), (0, padding)))
        both = both.reshape(2, 2, e_local, groups, tile_width)
        both = both.transpose(3, 0, 1, 2, 4).reshape(groups, 4 * e_local, tile_width)
    got = lax.all_to_all(both, "energy", 0, 0, tiled=True)
    polar_tile = correlate(got.reshape(groups * 4 * e_local, tile_width), forward, inverse)

    send = polar_tile.reshape(groups, 2 * e_local, tile_width)
    back = lax.all_to_all(send, "energy", 0, 0, tiled=True)
    back_above = shifted(back, "space", -1)

    def as_blocks(received):
        received = received.reshape(groups, 2, e_local, tile_width).transpose(1, 2, 0, 3)
        received = received.reshape(2, e_local, groups * tile_width)[:, :, :elements]
        return received.reshape(2, e_local, BS, BS)

    polar = as_blocks(back)
    polar_above = as_blocks(back_above)
    diag_block = v_diag[0]
    to_next = sandwich(couple_own.T, polar, couple_own)
    from_below = shifted(to_next, "space", 1)
    local = lax.optimization_barrier(sandwich(diag_block, polar, diag_block))
    from_above = sandwich(couple_own, polar_above, couple_own.T)
    total = from_above + (local + from_below)
    return total.reshape(1, 2, e_local, elements)


def solution(mesh):
    placed = (
        P("space", None, "energy", None),
        P("space", None, "energy", None),
        P("space", None, None),
        P("space", None, None),
    )
    return jax.shard_map(
        per_device,
        mesh=mesh,
        in_specs=placed,
        out_specs=P("space", None, "energy", None),
        check_vma=False,
    )
```
